32 devices in a mesh: groups: 2 (over y), seq: 16 (over z, x, core).
Axes of the slice: x: 2, y: 2, z: 4, core: 2. Of those that a mesh axis runs over, the one named last changes fastest.
Arguments:
- left_stream: bfloat16 [4096, 4096], P(('groups', 'seq')), parts along dimension 0, may hold values from -6 to 6
- right_stream: bfloat16 [4096, 4096], P(('groups', 'seq')), parts along dimension 0, may hold values from -6 to 6
- gate_stream: bfloat16 [4096, 4096], P(('groups', 'seq')), parts along dimension 0, may hold values from -6 to 6
- filter_taps: bfloat16 [2048, 4096], P('seq'), may hold values from -1 to 1
- w_query: bfloat16 [4096, 128], replicated, may hold values from -8 to 8
- w_key: bfloat16 [4096, 128], replicated, may hold values from -1 to 1
- w_value: bfloat16 [4096, 128], replicated, may hold values from -0.09375 to 0.09375
Outputs:
- conv_out: bfloat16 [4096, 4096], P(('groups', 'seq')), parts along dimension 0
- attended: bfloat16 [4096, 128], P(('groups', 'seq')), parts along dimension 0
The draws below stay inside these ranges and needn't reach their ends.
There are 2 independent parts, one for each index of `groups`. The reference program is written for one: setup_inputs(seed, part) draws one part's arguments, and reference() takes and returns one part's arrays. A program takes and returns all parts, laid end to end along the dimension named above; an argument that names none is the same for every part. Nothing has to cross between parts.
All inputs are finite; a program needn't handle non-finite values.
Results may differ from the reference program's by a relative error of at most 0.012.
Values may be sent and summed in bfloat16 or wider, within the bound.
No kernel may reach another device: no remote copies, remote signals or barrier semaphores. Data moves between devices by JAX's collectives and lax.ppermute only.
A program may use at most 128 MiB of HBM per device.

```python
import math
import jax
import jax.numpy as jnp
from jax import lax

C = 4096
HD = 128
TOKENS = 2048


def draw_filter_taps(key, part):
    key_rate = jax.random.fold_in(key, 21)
    key_rough = jax.random.fold_in(key, 22)
    decay = jnp.exp(jax.random.uniform(key_rate, (1, C), jnp.float32, math.log(40.0), math.log(TOKENS * 4.0)))
    rough = jnp.clip(jax.random.normal(key_rough, (TOKENS, C), jnp.float32), -4.0, 4.0)
    position = jnp.arange(TOKENS, dtype=jnp.float32)[:, None]
    gain = jax.lax.rsqrt(0.5 * jnp.minimum(decay, TOKENS * 1.0))
    return (gain * jnp.exp(-position / decay) * rough).astype(jnp.bfloat16)


def shared_weight(key):
    raw = jax.random.normal(jax.random.fold_in(key, 31), (C, HD), jnp.float32)
    return jnp.clip(raw, -3.0, 3.0) * C ** (-0.5)


def draw_w_key(key, part):
    return shared_weight(key).astype(jnp.bfloat16)


def draw_w_query(key, part):
    own = jnp.clip(jax.random.normal(jax.random.fold_in(key, 32), (C, HD), jnp.float32), -3.0, 3.0) * C ** (-0.5)
    return own.astype(jnp.bfloat16)


def levels(key, shape, split, smallest, largest):
    loudness, own = 1.0, jax.random.fold_in(key, 6)
    for axis_at, blocks in split:
        heights = jnp.exp(jax.random.uniform(jax.random.fold_in(own, axis_at), (blocks,), jnp.float32, smallest / len(split), largest / len(split)))
        loudness = loudness * jnp.repeat(heights, shape[axis_at] // blocks).reshape([-1 if axis == axis_at else 1 for axis in range(len(shape))])
    return loudness


def noise(rng, extent, spread, reach, pieces=(), kind=jnp.bfloat16):
    loudness = levels(rng, extent, pieces, -0.22, 0.18) if pieces else 1.0
    drawn = jax.random.normal(rng, extent, jnp.float32) * spread * loudness
    return jnp.minimum(jnp.maximum(drawn, -reach), reach).astype(kind)


def setup_inputs(seed: int = 0, part: int = 0) -> dict:
    splits = jax.random.split(jax.random.key(seed), 8)
    part_keys = jax.random.split(jax.random.fold_in(splits[7], part), 8)
    return {
        "left_stream": noise(part_keys[0], (TOKENS, C), 1.0, 6.0, ((0, 16),)),
        "right_stream": noise(part_keys[1], (TOKENS, C), 1.0, 6.0, ((0, 16),)),
        "gate_stream": noise(part_keys[2], (TOKENS, C), 1.0, 6.0, ((0, 16),)),
        "filter_taps": draw_filter_taps(jax.random.fold_in(splits[7], 71), part),
        "w_query": draw_w_query(jax.random.fold_in(splits[7], 71), part),
        "w_key": draw_w_key(jax.random.fold_in(splits[7], 71), part),
        "w_value": noise(splits[6], (C, HD), C ** -0.5, 0.09375),
    }


def convolve_block(pair):
    signal, taps = pair
    length = signal.shape[1]
    spec_a = jnp.fft.rfft(signal, n=2 * length, axis=1)
    spec_b = jnp.fft.rfft(taps, n=2 * length, axis=1)
    result = jnp.fft.irfft(spec_a * spec_b, n=2 * length, axis=1)[:, :length]
    return result.astype(jnp.float32)

def reference(left_stream, right_stream, gate_stream, filter_taps, w_query, w_key, w_value):
    mixed = (left_stream.astype(jnp.float32) * right_stream.astype(jnp.float32)).astype(jnp.bfloat16)
    length = mixed.shape[0]
    block = math.gcd(C, 128)
    signal = mixed.astype(jnp.float32).T.reshape(C // block, block, length)
    taps = filter_taps.astype(jnp.float32).T.reshape(C // block, block, length)
    long_part = lax.map(convolve_block, (signal, taps)).reshape(C, length).T
    conv_out = (gate_stream.astype(jnp.float32) * long_part).astype(jnp.bfloat16)
    query = jnp.dot(conv_out, w_query, preferred_element_type=jnp.float32).astype(jnp.bfloat16)
    key = jnp.dot(conv_out, w_key, preferred_element_type=jnp.float32).astype(jnp.bfloat16)
    value = jnp.dot(conv_out, w_value, preferred_element_type=jnp.float32).astype(jnp.bfloat16)
    scale = 1.0 / math.sqrt(HD)
    qblock = math.gcd(length, 512)
    count = length // qblock
    blocks = query.reshape(count, qblock, HD)
    starts = jnp.arange(count, dtype=jnp.int32) * qblock
    key_pos = jnp.arange(length, dtype=jnp.int32)

    def rows_of(args):
        block_q, start = args
        score = jnp.dot(block_q, key.T, preferred_element_type=jnp.float32) * scale
        query_pos = start + jnp.arange(qblock, dtype=jnp.int32)
        allowed = key_pos[None, :] <= query_pos[:, None]
        masked = jnp.where(allowed, score, -1e+30)
        peak = lax.optimization_barrier(jnp.max(masked, axis=1))
        weight = jnp.where(allowed, jnp.exp(masked - peak[:, None]), 0.0)
        total = lax.optimization_barrier(jnp.sum(weight, axis=1))
        summed = jnp.dot(weight.astype(jnp.bfloat16), value, preferred_element_type=jnp.float32)
        return (summed / total[:, None]).astype(jnp.bfloat16)
    attended = lax.map(rows_of, (blocks, starts)).reshape(length, HD)
    return (conv_out, attended)
```

```python
import math

import jax
import jax.numpy as jnp
from jax import lax
from jax.sharding import PartitionSpec as P

careful = lax.Precision.HIGH


def angle_table(rows, cols, period, sign):
    product = (
        lax.broadcasted_iota(jnp.int32, (rows, cols), 0)
        * lax.broadcasted_iota(jnp.int32, (rows, cols), 1)
        % period
    )
    phase = product.astype(jnp.float32) * (sign * 2.0 * math.pi / period)
    return (jnp.cos(phase), jnp.sin(phase))


def spectrum(signal):
    count, half, width = signal.shape
    outer = 2 * half
    whole = outer * width
    cos_a, sin_a = angle_table(outer, half, outer, -1.0)
    real_a = jnp.einsum(
        "kn,cnm->ckm", cos_a, signal, precision=careful, preferred_element_type=jnp.float32
    )
    imag_a = jnp.einsum(
        "kn,cnm->ckm", sin_a, signal, precision=careful, preferred_element_type=jnp.float32
    )
    cos_t, sin_t = angle_table(outer, width, whole, -1.0)
    real_b = real_a * cos_t - imag_a * sin_t
    imag_b = real_a * sin_t + imag_a * cos_t
    cos_c, sin_c = angle_table(width, width, width, -1.0)
    real_x = jnp.einsum("cqn,kn->cqk", real_b, cos_c, precision=careful) - jnp.einsum(
        "cqn,kn->cqk", imag_b, sin_c, precision=careful
    )
    imag_x = jnp.einsum("cqn,kn->cqk", real_b, sin_c, precision=careful) + jnp.einsum(
        "cqn,kn->cqk", imag_b, cos_c, precision=careful
    )
    return (real_x, imag_x)


def inverse_real(real_y, imag_y, half):
    count, outer, width = real_y.shape
    whole = outer * width
    cos_c, sin_c = angle_table(width, width, width, 1.0)
    real_c = jnp.einsum("cqk,kn->cqn", real_y, cos_c, precision=careful) - jnp.einsum(
        "cqk,kn->cqn", imag_y, sin_c, precision=careful
    )
    imag_c = jnp.einsum("cqk,kn->cqn", real_y, sin_c, precision=careful) + jnp.einsum(
        "cqk,kn->cqn", imag_y, cos_c, precision=careful
    )
    cos_t, sin_t = angle_table(outer, width, whole, 1.0)
    real_d = real_c * cos_t - imag_c * sin_t
    imag_d = real_c * sin_t + imag_c * cos_t
    cos_a, sin_a = angle_table(half, outer, outer, 1.0)
    result = jnp.einsum("nk,ckm->cnm", cos_a, real_d, precision=careful) - jnp.einsum(
        "nk,ckm->cnm", sin_a, imag_d, precision=careful
    )
    return (result / whole).reshape(count, half * width)


def make_convolver(width, pieces):
    signal = pieces[0]
    taps = pieces[1]
    count = signal.shape[1]
    length = signal.shape[2]
    half = length // width
    sig_real, sig_imag = spectrum(signal.reshape(count, half, width))
    tap_real, tap_imag = spectrum(taps.reshape(count, half, width))
    prod_real = sig_real * tap_real - sig_imag * tap_imag
    prod_imag = sig_real * tap_imag + sig_imag * tap_real
    long_part = inverse_real(prod_real, prod_imag, half).reshape(1, count, length)
    return long_part


def gather_earlier(block, shards, me):
    plane = 4 if shards % 4 == 0 else 1
    lines = shards // plane
    lane = me % plane
    level = me // plane
    forward = [(i, i + plane) for i in range(shards - plane)]
    current = block
    stack = [block]
    for _ in range(lines - 1):
        current = lax.ppermute(current, "seq", forward)
        stack.append(current)
    stack = jnp.stack(stack)
    depth = jnp.arange(lines, dtype=jnp.int32)
    src_level = level - depth
    parts = [stack]
    srcs = [jnp.where(src_level >= 0, src_level * plane + lane, shards)]
    for shift in range(1, plane):
        perm = [
            (p * plane + l, p * plane + (l + shift) % plane)
            for p in range(lines)
            for l in range(plane)
        ]
        parts.append(lax.ppermute(stack, "seq", perm))
        from_lane = (lane - shift) % plane
        srcs.append(jnp.where(src_level >= 0, src_level * plane + from_lane, shards))
    return jnp.concatenate(parts), jnp.concatenate(srcs)


def on_device(left_stream, right_stream, gate_stream, filter_taps, w_query, w_key, w_value):
    rows, channels = left_stream.shape
    shards = lax.axis_size("seq")
    group = channels // shards
    mixed = (left_stream.astype(jnp.float32) * right_stream.astype(jnp.float32)).astype(
        jnp.bfloat16
    )
    mixed_groups = mixed.T.reshape(shards, group, rows)
    tap_groups = filter_taps.T.reshape(shards, group, rows)
    long_groups = make_convolver(
        rows,
        (
            lax.all_to_all(mixed_groups, "seq", split_axis=0, concat_axis=2, tiled=True),
            lax.all_to_all(tap_groups, "seq", split_axis=0, concat_axis=2, tiled=True),
        ),
    )
    returned = lax.all_to_all(
        long_groups.astype(jnp.bfloat16), "seq", split_axis=2, concat_axis=0, tiled=True
    )
    long_part = returned.reshape(channels, rows).T.astype(jnp.float32)
    conv_out = (gate_stream.astype(jnp.float32) * long_part).astype(jnp.bfloat16)
    query = jnp.dot(conv_out, w_query, preferred_element_type=jnp.float32).astype(jnp.bfloat16)
    key = jnp.dot(conv_out, w_key, preferred_element_type=jnp.float32).astype(jnp.bfloat16)
    value = jnp.dot(conv_out, w_value, preferred_element_type=jnp.float32).astype(jnp.bfloat16)
    head_size = w_query.shape[1]
    scale = 1.0 / math.sqrt(head_size)
    me = lax.axis_index("seq")
    query_pos = me * rows + jnp.arange(rows, dtype=jnp.int32)
    pairs = jnp.concatenate([key, value], axis=1)
    blocks, sources = gather_earlier(pairs, shards, me)
    keys = blocks[:, :, :head_size].reshape(-1, head_size)
    values = blocks[:, :, head_size:].reshape(-1, head_size)
    key_pos = (sources[:, None] * rows + jnp.arange(rows, dtype=jnp.int32)[None, :]).reshape(-1)
    score = jnp.einsum("qd,kd->qk", query, keys, preferred_element_type=jnp.float32) * scale
    allowed = key_pos[None, :] <= query_pos[:, None]
    masked = jnp.where(allowed, score, -1e30)
    peak = jnp.max(masked, axis=1)
    weight = jnp.where(allowed, jnp.exp(masked - peak[:, None]), 0.0)
    total = jnp.sum(weight, axis=1)
    summed = jnp.dot(weight.astype(jnp.bfloat16), values, preferred_element_type=jnp.float32)
    attended = (summed / total[:, None]).astype(jnp.bfloat16)
    return (conv_out, attended)


def solution(mesh):
    in_specs = (
        P(("groups", "seq"), None),
        P(("groups", "seq"), None),
        P(("groups", "seq"), None),
        P("seq", None),
        P(),
        P(),
        P(),
    )
    out_specs = (P(("groups", "seq"), None), P(("groups", "seq"), None))
    return jax.shard_map(
        on_device, mesh=mesh, in_specs=in_specs, out_specs=out_specs, check_vma=False
    )
```

```python
import math

import jax
import jax.numpy as jnp
from jax import lax
from jax.sharding import PartitionSpec as P

careful = lax.Precision.HIGH


def angle_table(rows, cols, period, sign):
    product = (
        lax.broadcasted_iota(jnp.int32, (rows, cols), 0)
        * lax.broadcasted_iota(jnp.int32, (rows, cols), 1)
        % period
    )
    phase = product.astype(jnp.float32) * (sign * 2.0 * math.pi / period)
    return (jnp.cos(phase), jnp.sin(phase))


def spectrum(signal):
    count, half, width = signal.shape
    outer = 2 * half
    whole = outer * width
    cos_a, sin_a = angle_table(outer, half, outer, -1.0)
    real_a = jnp.einsum(
        "kn,cnm->ckm", cos_a, signal, precision=careful, preferred_element_type=jnp.float32
    )
    imag_a = jnp.einsum(
        "kn,cnm->ckm", sin_a, signal, precision=careful, preferred_element_type=jnp.float32
    )
    cos_t, sin_t = angle_table(outer, width, whole, -1.0)
    real_b = real_a * cos_t - imag_a * sin_t
    imag_b = real_a * sin_t + imag_a * cos_t
    cos_c, sin_c = angle_table(width, width, width, -1.0)
    real_x = jnp.einsum("cqn,kn->cqk", real_b, cos_c, precision=careful) - jnp.einsum(
        "cqn,kn->cqk", imag_b, sin_c, precision=careful
    )
    imag_x = jnp.einsum("cqn,kn->cqk", real_b, sin_c, precision=careful) + jnp.einsum(
        "cqn,kn->cqk", imag_b, cos_c, precision=careful
    )
    return (real_x, imag_x)


def inverse_real(real_y, imag_y, half):
    count, outer, width = real_y.shape
    whole = outer * width
    cos_c, sin_c = angle_table(width, width, width, 1.0)
    real_c = jnp.einsum("cqk,kn->cqn", real_y, cos_c, precision=careful) - jnp.einsum(
        "cqk,kn->cqn", imag_y, sin_c, precision=careful
    )
    imag_c = jnp.einsum("cqk,kn->cqn", real_y, sin_c, precision=careful) + jnp.einsum(
        "cqk,kn->cqn", imag_y, cos_c, precision=careful
    )
    cos_t, sin_t = angle_table(outer, width, whole, 1.0)
    real_d = real_c * cos_t - imag_c * sin_t
    imag_d = real_c * sin_t + imag_c * cos_t
    cos_a, sin_a = angle_table(half, outer, outer, 1.0)
    result = jnp.einsum("nk,ckm->cnm", cos_a, real_d, precision=careful) - jnp.einsum(
        "nk,ckm->cnm", sin_a, imag_d, precision=careful
    )
    return (result / whole).reshape(count, half * width)


def make_convolver(width, pieces):
    signal = pieces[0]
    taps = pieces[1]
    count = signal.shape[1]
    length = signal.shape[2]
    half = length // width
    sig_real, sig_imag = spectrum(signal.reshape(count, half, width))
    tap_real, tap_imag = spectrum(taps.reshape(count, half, width))
    prod_real = sig_real * tap_real - sig_imag * tap_imag
    prod_imag = sig_real * tap_imag + sig_imag * tap_real
    long_part = inverse_real(prod_real, prod_imag, half).reshape(1, count, length)
    return long_part


def gather_earlier(block, shards, me):
    plane = 4 if shards % 4 == 0 else 1
    lines = shards // plane
    lane = me % plane
    level = me // plane
    forward = [(i, i + plane) for i in range(shards - plane)]
    current = block
    stack = [block]
    for _ in range(lines - 1):
        current = lax.ppermute(current, "seq", forward)
        stack.append(current)
    stack = jnp.stack(stack)
    depth = jnp.arange(lines, dtype=jnp.int32)
    src_level = level - depth
    parts = [stack]
    srcs = [jnp.where(src_level >= 0, src_level * plane + lane, shards)]
    for shift in range(1, plane):
        perm = [
            (p * plane + l, p * plane + (l + shift) % plane)
            for p in range(lines)
            for l in range(plane)
        ]
        parts.append(lax.ppermute(stack, "seq", perm))
        from_lane = (lane - shift) % plane
        srcs.append(jnp.where(src_level >= 0, src_level * plane + from_lane, shards))
    return jnp.concatenate(parts), jnp.concatenate(srcs)


def on_device(left_stream, right_stream, gate_stream, filter_taps, w_query, w_key, w_value):
    rows, channels = left_stream.shape
    shards = lax.axis_size("seq")
    group = channels // shards
    mixed = (left_stream.astype(jnp.float32) * right_stream.astype(jnp.float32)).astype(
        jnp.bfloat16
    )
    mixed_groups = mixed.T.reshape(shards, group, rows)
    tap_groups = filter_taps.T.reshape(shards, group, rows)
    long_groups = make_convolver(
        rows,
        (
            lax.all_to_all(mixed_groups, "seq", split_axis=0, concat_axis=2, tiled=True),
            lax.all_to_all(tap_groups, "seq", split_axis=0, concat_axis=2, tiled=True),
        ),
    )
    outgoing = long_groups.reshape(group, shards, rows).transpose(1, 0, 2).astype(jnp.bfloat16)
    returned = lax.all_to_all(outgoing, "seq", split_axis=0, concat_axis=0, tiled=True)
    long_part = returned.reshape(channels, rows).T.astype(jnp.float32)
    conv_out = (gate_stream.astype(jnp.float32) * long_part).astype(jnp.bfloat16)
    query = jnp.dot(conv_out, w_query, preferred_element_type=jnp.float32).astype(jnp.bfloat16)
    key = jnp.dot(conv_out, w_key, preferred_element_type=jnp.float32).astype(jnp.bfloat16)
    value = jnp.dot(conv_out, w_value, preferred_element_type=jnp.float32).astype(jnp.bfloat16)
    head_size = w_query.shape[1]
    scale = 1.0 / math.sqrt(head_size)
    me = lax.axis_index("seq")
    query_pos = me * rows + jnp.arange(rows, dtype=jnp.int32)
    pairs = jnp.concatenate([key, value], axis=1)
    blocks, sources = gather_earlier(pairs, shards, me)
    keys = blocks[:, :, :head_size].reshape(-1, head_size)
    values = blocks[:, :, head_size:].reshape(-1, head_size)
    key_pos = (sources[:, None] * rows + jnp.arange(rows, dtype=jnp.int32)[None, :]).reshape(-1)
    score = jnp.einsum("qd,kd->qk", query, keys, preferred_element_type=jnp.float32) * scale
    allowed = key_pos[None, :] <= query_pos[:, None]
    masked = jnp.where(allowed, score, -1e30)
    peak = jnp.max(masked, axis=1)
    weight = jnp.where(allowed, jnp.exp(masked - peak[:, None]), 0.0)
    total = jnp.sum(weight, axis=1)
    summed = jnp.dot(weight.astype(jnp.bfloat16), values, preferred_element_type=jnp.float32)
    attended = (summed / total[:, None]).astype(jnp.bfloat16)
    return (conv_out, attended)


def solution(mesh):
    in_specs = (
        P(("groups", "seq"), None),
        P(("groups", "seq"), None),
        P(("groups", "seq"), None),
        P("seq", None),
        P(),
        P(),
        P(),
    )
    out_specs = (P(("groups", "seq"), None), P(("groups", "seq"), None))
    return jax.shard_map(
        on_device, mesh=mesh, in_specs=in_specs, out_specs=out_specs, check_vma=False
    )
```

```python
import math

import jax
import jax.numpy as jnp
from jax import lax
from jax.sharding import PartitionSpec as P

careful = lax.Precision.HIGH


def angle_table(rows, cols, period, sign):
    product = (
        lax.broadcasted_iota(jnp.int32, (rows, cols), 0)
        * lax.broadcasted_iota(jnp.int32, (rows, cols), 1)
        % period
    )
    phase = product.astype(jnp.float32) * (sign * 2.0 * math.pi / period)
    return (jnp.cos(phase), jnp.sin(phase))


def spectrum(signal):
    count, half, width = signal.shape
    outer = 2 * half
    whole = outer * width
    cos_a, sin_a = angle_table(outer, half, outer, -1.0)
    real_a = jnp.einsum(
        "kn,cnm->ckm", cos_a, signal, precision=careful, preferred_element_type=jnp.float32
    )
    imag_a = jnp.einsum(
        "kn,cnm->ckm", sin_a, signal, precision=careful, preferred_element_type=jnp.float32
    )
    cos_t, sin_t = angle_table(outer, width, whole, -1.0)
    real_b = real_a * cos_t - imag_a * sin_t
    imag_b = real_a * sin_t + imag_a * cos_t
    cos_c, sin_c = angle_table(width, width, width, -1.0)
    real_x = jnp.einsum("cqn,kn->cqk", real_b, cos_c, precision=careful) - jnp.einsum(
        "cqn,kn->cqk", imag_b, sin_c, precision=careful
    )
    imag_x = jnp.einsum("cqn,kn->cqk", real_b, sin_c, precision=careful) + jnp.einsum(
        "cqn,kn->cqk", imag_b, cos_c, precision=careful
    )
    return (real_x, imag_x)


def inverse_real(real_y, imag_y, half):
    count, outer, width = real_y.shape
    whole = outer * width
    cos_c, sin_c = angle_table(width, width, width, 1.0)
    real_c = jnp.einsum("cqk,kn->cqn", real_y, cos_c, precision=careful) - jnp.einsum(
        "cqk,kn->cqn", imag_y, sin_c, precision=careful
    )
    imag_c = jnp.einsum("cqk,kn->cqn", real_y, sin_c, precision=careful) + jnp.einsum(
        "cqk,kn->cqn", imag_y, cos_c, precision=careful
    )
    cos_t, sin_t = angle_table(outer, width, whole, 1.0)
    real_d = real_c * cos_t - imag_c * sin_t
    imag_d = real_c * sin_t + imag_c * cos_t
    cos_a, sin_a = angle_table(half, outer, outer, 1.0)
    result = jnp.einsum("nk,ckm->cnm", cos_a, real_d, precision=careful) - jnp.einsum(
        "nk,ckm->cnm", sin_a, imag_d, precision=careful
    )
    return (result / whole).reshape(count, half * width)


def make_convolver(width, pieces, waits=None):
    signal = pieces[0]
    taps = pieces[1]
    count = signal.shape[1]
    length = signal.shape[2]
    half = length // width
    sig_real, sig_imag = spectrum(signal.reshape(count, half, width))
    tap_real, tap_imag = spectrum(taps.reshape(count, half, width))
    prod_real = sig_real * tap_real - sig_imag * tap_imag
    prod_imag = sig_real * tap_imag + sig_imag * tap_real
    if waits is not None:
        prod_real, prod_imag, waits = lax.optimization_barrier((prod_real, prod_imag, waits))
    long_part = inverse_real(prod_real, prod_imag, half).reshape(1, count, length)
    return long_part, waits


def gather_earlier(block, shards, me):
    plane = 4 if shards % 4 == 0 else 1
    lines = shards // plane
    lane = me % plane
    level = me // plane
    stack = [block]
    for depth in range(1, lines):
        step = depth * plane
        stack.append(lax.ppermute(block, "seq", [(i, i + step) for i in range(shards - step)]))
    stack = jnp.stack(stack)
    src_level = level - jnp.arange(lines, dtype=jnp.int32)

    def origin(from_lane):
        return jnp.where(src_level >= 0, src_level * plane + from_lane, shards)

    if plane == 1:
        return stack, origin(lane)
    base = [p * plane for p in range(lines)]
    across = [(b + l, b + (l ^ 2)) for b in base for l in range(plane)]
    beside = [(b + l, b + (l ^ 1)) for b in base for l in range(plane)]
    far = lax.ppermute(stack, "seq", across)
    both = jnp.concatenate([stack, far])
    near = lax.ppermute(both, "seq", beside)
    blocks = jnp.concatenate([both, near])
    sources = jnp.concatenate(
        [origin(lane), origin(lane ^ 2), origin(lane ^ 1), origin(lane ^ 3)]
    )
    return blocks, sources

def on_device(left_stream, right_stream, gate_stream, filter_taps, w_query, w_key, w_value):
    rows, channels = left_stream.shape
    shards = lax.axis_size("seq")
    group = channels // shards
    mixed = (left_stream.astype(jnp.float32) * right_stream.astype(jnp.float32)).astype(
        jnp.bfloat16
    )
    mixed_groups = mixed.T.reshape(shards, group, rows)
    tap_groups = filter_taps.T.reshape(shards, group, rows)
    chunks = 2 if group % 16 == 0 else 1
    sub = group // chunks
    gate_groups = gate_stream.T.reshape(shards, group, rows)
    arrived = []
    for k in range(chunks):
        cut = slice(k * sub, (k + 1) * sub)
        parts = [mixed_groups[:, cut], tap_groups[:, cut]]
        if k == chunks - 1:
            parts.append(gate_groups)
        payload = jnp.concatenate(parts, axis=1)
        arrived.append(lax.all_to_all(payload, "seq", split_axis=0, concat_axis=2, tiled=True))
    gates = arrived[-1][:, 2 * sub :].astype(jnp.float32)
    pieces = []
    previous = None
    for k in range(chunks):
        got = arrived[k]
        back = None
        if previous is not None:
            got, previous = lax.optimization_barrier((got, previous))
            back = lax.all_to_all(previous, "seq", split_axis=0, concat_axis=0, tiled=True)
        long_k, back = make_convolver(rows, (got[:, :sub], got[:, sub : 2 * sub]), back)
        if back is not None:
            pieces.append(back)
        conv_k = (gates[:, k * sub : (k + 1) * sub] * long_k).astype(jnp.bfloat16)
        previous = conv_k.reshape(sub, shards, rows).transpose(1, 0, 2)
    pieces.append(lax.all_to_all(previous, "seq", split_axis=0, concat_axis=0, tiled=True))
    returned = jnp.concatenate(pieces, axis=1)
    conv_out = returned.reshape(channels, rows).T
    query = jnp.dot(conv_out, w_query, preferred_element_type=jnp.float32).astype(jnp.bfloat16)
    key = jnp.dot(conv_out, w_key, preferred_element_type=jnp.float32).astype(jnp.bfloat16)
    value = jnp.dot(conv_out, w_value, preferred_element_type=jnp.float32).astype(jnp.bfloat16)
    head_size = w_query.shape[1]
    scale = 1.0 / math.sqrt(head_size)
    me = lax.axis_index("seq")
    query_pos = me * rows + jnp.arange(rows, dtype=jnp.int32)
    pairs = jnp.concatenate([key, value], axis=1)
    blocks, sources = gather_earlier(pairs, shards, me)
    keys = blocks[:, :, :head_size].reshape(-1, head_size)
    values = blocks[:, :, head_size:].reshape(-1, head_size)
    key_pos = (sources[:, None] * rows + jnp.arange(rows, dtype=jnp.int32)[None, :]).reshape(-1)
    score = jnp.einsum("qd,kd->qk", query, keys, preferred_element_type=jnp.float32) * scale
    allowed = key_pos[None, :] <= query_pos[:, None]
    masked = jnp.where(allowed, score, -1e30)
    peak = jnp.max(masked, axis=1)
    weight = jnp.where(allowed, jnp.exp(masked - peak[:, None]), 0.0)
    total = jnp.sum(weight, axis=1)
    summed = jnp.dot(weight.astype(jnp.bfloat16), values, preferred_element_type=jnp.float32)
    attended = (summed / total[:, None]).astype(jnp.bfloat16)
    return (conv_out, attended)


def solution(mesh):
    in_specs = (
        P(("groups", "seq"), None),
        P(("groups", "seq"), None),
        P(("groups", "seq"), None),
        P("seq", None),
        P(),
        P(),
        P(),
    )
    out_specs = (P(("groups", "seq"), None), P(("groups", "seq"), None))
    return jax.shard_map(
        on_device, mesh=mesh, in_specs=in_specs, out_specs=out_specs, check_vma=False
    )
```

```python
import math

import jax
import jax.numpy as jnp
from jax import lax
from jax.sharding import PartitionSpec as P

careful = lax.Precision.HIGH


def angle_table(rows, cols, period, sign):
    product = (
        lax.broadcasted_iota(jnp.int32, (rows, cols), 0)
        * lax.broadcasted_iota(jnp.int32, (rows, cols), 1)
        % period
    )
    phase = product.astype(jnp.float32) * (sign * 2.0 * math.pi / period)
    return (jnp.cos(phase), jnp.sin(phase))


def spectrum(signal):
    count, half, width = signal.shape
    outer = 2 * half
    whole = outer * width
    cos_a, sin_a = angle_table(outer, half, outer, -1.0)
    real_a = jnp.einsum(
        "kn,cnm->ckm", cos_a, signal, precision=careful, preferred_element_type=jnp.float32
    )
    imag_a = jnp.einsum(
        "kn,cnm->ckm", sin_a, signal, precision=careful, preferred_element_type=jnp.float32
    )
    cos_t, sin_t = angle_table(outer, width, whole, -1.0)
    real_b = real_a * cos_t - imag_a * sin_t
    imag_b = real_a * sin_t + imag_a * cos_t
    cos_c, sin_c = angle_table(width, width, width, -1.0)
    real_x = jnp.einsum("cqn,kn->cqk", real_b, cos_c, precision=careful) - jnp.einsum(
        "cqn,kn->cqk", imag_b, sin_c, precision=careful
    )
    imag_x = jnp.einsum("cqn,kn->cqk", real_b, sin_c, precision=careful) + jnp.einsum(
        "cqn,kn->cqk", imag_b, cos_c, precision=careful
    )
    return (real_x, imag_x)


def inverse_real(real_y, imag_y, half):
    count, outer, width = real_y.shape
    whole = outer * width
    cos_c, sin_c = angle_table(width, width, width, 1.0)
    real_c = jnp.einsum("cqk,kn->cqn", real_y, cos_c, precision=careful) - jnp.einsum(
        "cqk,kn->cqn", imag_y, sin_c, precision=careful
    )
    imag_c = jnp.einsum("cqk,kn->cqn", real_y, sin_c, precision=careful) + jnp.einsum(
        "cqk,kn->cqn", imag_y, cos_c, precision=careful
    )
    cos_t, sin_t = angle_table(outer, width, whole, 1.0)
    real_d = real_c * cos_t - imag_c * sin_t
    imag_d = real_c * sin_t + imag_c * cos_t
    cos_a, sin_a = angle_table(half, outer, outer, 1.0)
    result = jnp.einsum("nk,ckm->cnm", cos_a, real_d, precision=careful) - jnp.einsum(
        "nk,ckm->cnm", sin_a, imag_d, precision=careful
    )
    return (result / whole).reshape(count, half * width)


def make_convolver(width, pieces, waits=None):
    signal = pieces[0]
    taps = pieces[1]
    count = signal.shape[1]
    length = signal.shape[2]
    half = length // width
    sig_real, sig_imag = spectrum(signal.reshape(count, half, width))
    tap_real, tap_imag = spectrum(taps.reshape(count, half, width))
    prod_real = sig_real * tap_real - sig_imag * tap_imag
    prod_imag = sig_real * tap_imag + sig_imag * tap_real
    if waits is not None:
        prod_real, prod_imag, waits = lax.optimization_barrier((prod_real, prod_imag, waits))
    long_part = inverse_real(prod_real, prod_imag, half).reshape(1, count, length)
    return long_part, waits


def gather_earlier(block, shards, me):
    plane = 4 if shards % 4 == 0 else 1
    lines = shards // plane
    lane = me % plane
    level = me // plane
    stack = [block]
    for depth in range(1, lines):
        step = depth * plane
        stack.append(lax.ppermute(block, "seq", [(i, i + step) for i in range(shards - step)]))
    stack = jnp.stack(stack)
    src_level = level - jnp.arange(lines, dtype=jnp.int32)

    def origin(from_lane):
        return jnp.where(src_level >= 0, src_level * plane + from_lane, shards)

    if plane == 1:
        return stack, origin(lane)
    base = [p * plane for p in range(lines)]
    across = [(b + l, b + (l ^ 2)) for b in base for l in range(plane)]
    beside = [(b + l, b + (l ^ 1)) for b in base for l in range(plane)]
    far = lax.ppermute(stack, "seq", across)
    both = jnp.concatenate([stack, far])
    near = lax.ppermute(both, "seq", beside)
    blocks = jnp.concatenate([both, near])
    sources = jnp.concatenate(
        [origin(lane), origin(lane ^ 2), origin(lane ^ 1), origin(lane ^ 3)]
    )
    return blocks, sources

def on_device(left_stream, right_stream, gate_stream, filter_taps, w_query, w_key, w_value):
    rows, channels = left_stream.shape
    shards = lax.axis_size("seq")
    group = channels // shards
    mixed = (left_stream.astype(jnp.float32) * right_stream.astype(jnp.float32)).astype(
        jnp.bfloat16
    )
    mixed_groups = mixed.T.reshape(shards, group, rows)
    tap_groups = filter_taps.T.reshape(shards, group, rows)
    chunks = 1
    sub = group // chunks
    gate_groups = gate_stream.T.reshape(shards, group, rows)
    arrived = []
    for k in range(chunks):
        cut = slice(k * sub, (k + 1) * sub)
        payload = jnp.concatenate([mixed_groups[:, cut], tap_groups[:, cut]], axis=1)
        arrived.append(lax.all_to_all(payload, "seq", split_axis=0, concat_axis=2, tiled=True))
    gates = lax.all_to_all(gate_groups, "seq", split_axis=0, concat_axis=2, tiled=True)
    pieces = []
    previous = None
    for k in range(chunks):
        got = arrived[k]
        back = None
        if previous is not None:
            got, previous = lax.optimization_barrier((got, previous))
            back = lax.all_to_all(previous, "seq", split_axis=0, concat_axis=0, tiled=True)
        long_k, back = make_convolver(rows, (got[:, :sub], got[:, sub : 2 * sub]), back)
        if back is not None:
            pieces.append(back)
        conv_k = (gates[:, k * sub : (k + 1) * sub].astype(jnp.float32) * long_k).astype(
            jnp.bfloat16
        )
        previous = conv_k.reshape(sub, shards, rows).transpose(1, 0, 2)
    pieces.append(lax.all_to_all(previous, "seq", split_axis=0, concat_axis=0, tiled=True))
    returned = jnp.concatenate(pieces, axis=1)
    conv_out = returned.reshape(channels, rows).T
    query = jnp.dot(conv_out, w_query, preferred_element_type=jnp.float32).astype(jnp.bfloat16)
    key = jnp.dot(conv_out, w_key, preferred_element_type=jnp.float32).astype(jnp.bfloat16)
    value = jnp.dot(conv_out, w_value, preferred_element_type=jnp.float32).astype(jnp.bfloat16)
    head_size = w_query.shape[1]
    scale = 1.0 / math.sqrt(head_size)
    me = lax.axis_index("seq")
    query_pos = me * rows + jnp.arange(rows, dtype=jnp.int32)
    pairs = jnp.concatenate([key, value], axis=1)
    blocks, sources = gather_earlier(pairs, shards, me)
    keys = blocks[:, :, :head_size].reshape(-1, head_size)
    values = blocks[:, :, head_size:].reshape(-1, head_size)
    key_pos = (sources[:, None] * rows + jnp.arange(rows, dtype=jnp.int32)[None, :]).reshape(-1)
    score = jnp.einsum("qd,kd->qk", query, keys, preferred_element_type=jnp.float32) * scale
    allowed = key_pos[None, :] <= query_pos[:, None]
    masked = jnp.where(allowed, score, -1e30)
    peak = jnp.max(masked, axis=1)
    weight = jnp.where(allowed, jnp.exp(masked - peak[:, None]), 0.0)
    total = jnp.sum(weight, axis=1)
    summed = jnp.dot(weight.astype(jnp.bfloat16), values, preferred_element_type=jnp.float32)
    attended = (summed / total[:, None]).astype(jnp.bfloat16)
    return (conv_out, attended)


def solution(mesh):
    in_specs = (
        P(("groups", "seq"), None),
        P(("groups", "seq"), None),
        P(("groups", "seq"), None),
        P("seq", None),
        P(),
        P(),
        P(),
    )
    out_specs = (P(("groups", "seq"), None), P(("groups", "seq"), None))
    return jax.shard_map(
        on_device, mesh=mesh, in_specs=in_specs, out_specs=out_specs, check_vma=False
    )
```

```python
import math

import jax
import jax.numpy as jnp
from jax import lax
from jax.sharding import PartitionSpec as P

careful = lax.Precision.HIGH


def angle_table(rows, cols, period, sign):
    product = (
        lax.broadcasted_iota(jnp.int32, (rows, cols), 0)
        * lax.broadcasted_iota(jnp.int32, (rows, cols), 1)
        % period
    )
    phase = product.astype(jnp.float32) * (sign * 2.0 * math.pi / period)
    return (jnp.cos(phase), jnp.sin(phase))


def spectrum(signal):
    count, half, width = signal.shape
    outer = 2 * half
    whole = outer * width
    cos_a, sin_a = angle_table(outer, half, outer, -1.0)
    real_a = jnp.einsum(
        "kn,cnm->ckm", cos_a, signal, precision=careful, preferred_element_type=jnp.float32
    )
    imag_a = jnp.einsum(
        "kn,cnm->ckm", sin_a, signal, precision=careful, preferred_element_type=jnp.float32
    )
    cos_t, sin_t = angle_table(outer, width, whole, -1.0)
    real_b = real_a * cos_t - imag_a * sin_t
    imag_b = real_a * sin_t + imag_a * cos_t
    cos_c, sin_c = angle_table(width, width, width, -1.0)
    real_x = jnp.einsum("cqn,kn->cqk", real_b, cos_c, precision=careful) - jnp.einsum(
        "cqn,kn->cqk", imag_b, sin_c, precision=careful
    )
    imag_x = jnp.einsum("cqn,kn->cqk", real_b, sin_c, precision=careful) + jnp.einsum(
        "cqn,kn->cqk", imag_b, cos_c, precision=careful
    )
    return (real_x, imag_x)


def inverse_real(real_y, imag_y, half):
    count, outer, width = real_y.shape
    whole = outer * width
    cos_c, sin_c = angle_table(width, width, width, 1.0)
    real_c = jnp.einsum("cqk,kn->cqn", real_y, cos_c, precision=careful) - jnp.einsum(
        "cqk,kn->cqn", imag_y, sin_c, precision=careful
    )
    imag_c = jnp.einsum("cqk,kn->cqn", real_y, sin_c, precision=careful) + jnp.einsum(
        "cqk,kn->cqn", imag_y, cos_c, precision=careful
    )
    cos_t, sin_t = angle_table(outer, width, whole, 1.0)
    real_d = real_c * cos_t - imag_c * sin_t
    imag_d = real_c * sin_t + imag_c * cos_t
    cos_a, sin_a = angle_table(half, outer, outer, 1.0)
    result = jnp.einsum("nk,ckm->cnm", cos_a, real_d, precision=careful) - jnp.einsum(
        "nk,ckm->cnm", sin_a, imag_d, precision=careful
    )
    return (result / whole).reshape(count, half * width)


def make_convolver(width, pieces, waits=None):
    signal = pieces[0]
    taps = pieces[1]
    count = signal.shape[1]
    length = signal.shape[2]
    half = length // width
    sig_real, sig_imag = spectrum(signal.reshape(count, half, width))
    tap_real, tap_imag = spectrum(taps.reshape(count, half, width))
    prod_real = sig_real * tap_real - sig_imag * tap_imag
    prod_imag = sig_real * tap_imag + sig_imag * tap_real
    if waits is not None:
        prod_real, prod_imag, waits = lax.optimization_barrier((prod_real, prod_imag, waits))
    long_part = inverse_real(prod_real, prod_imag, half).reshape(1, count, length)
    return long_part, waits


def gather_earlier(block, shards, me):
    plane = 4 if shards % 4 == 0 else 1
    lines = shards // plane
    lane = me % plane
    level = me // plane
    stack = [block]
    for depth in range(1, lines):
        step = depth * plane
        stack.append(lax.ppermute(block, "seq", [(i, i + step) for i in range(shards - step)]))
    stack = jnp.stack(stack)
    src_level = level - jnp.arange(lines, dtype=jnp.int32)

    def origin(from_lane):
        return jnp.where(src_level >= 0, src_level * plane + from_lane, shards)

    if plane == 1:
        return stack, origin(lane)
    base = [p * plane for p in range(lines)]
    across = [(b + l, b + (l ^ 2)) for b in base for l in range(plane)]
    beside = [(b + l, b + (l ^ 1)) for b in base for l in range(plane)]
    far = lax.ppermute(stack, "seq", across)
    both = jnp.concatenate([stack, far])
    near = lax.ppermute(both, "seq", beside)
    blocks = jnp.concatenate([both, near])
    sources = jnp.concatenate(
        [origin(lane), origin(lane ^ 2), origin(lane ^ 1), origin(lane ^ 3)]
    )
    return blocks, sources

def on_device(left_stream, right_stream, gate_stream, filter_taps, w_query, w_key, w_value):
    rows, channels = left_stream.shape
    shards = lax.axis_size("seq")
    group = channels // shards
    mixed = (left_stream.astype(jnp.float32) * right_stream.astype(jnp.float32)).astype(
        jnp.bfloat16
    )
    mixed_groups = mixed.T.reshape(shards, group, rows)
    tap_groups = filter_taps.T.reshape(shards, group, rows)
    chunks = 2 if group % 16 == 0 else 1
    sub = group // chunks
    arrived = []
    for k in range(chunks):
        cut = slice(k * sub, (k + 1) * sub)
        payload = jnp.concatenate([mixed_groups[:, cut], tap_groups[:, cut]], axis=1)
        arrived.append(lax.all_to_all(payload, "seq", split_axis=0, concat_axis=2, tiled=True))
    pieces = []
    previous = None
    for k in range(chunks):
        got = arrived[k]
        back = None
        if previous is not None:
            got, previous = lax.optimization_barrier((got, previous))
            back = lax.all_to_all(previous, "seq", split_axis=0, concat_axis=0, tiled=True)
        long_k, back = make_convolver(rows, (got[:, :sub], got[:, sub : 2 * sub]), back)
        if back is not None:
            pieces.append(back)
        previous = long_k.reshape(sub, shards, rows).transpose(1, 0, 2)
    pieces.append(lax.all_to_all(previous, "seq", split_axis=0, concat_axis=0, tiled=True))
    returned = jnp.concatenate(pieces, axis=1)
    long_part = returned.reshape(channels, rows).T
    conv_out = (gate_stream.astype(jnp.float32) * long_part).astype(jnp.bfloat16)
    query = jnp.dot(conv_out, w_query, preferred_element_type=jnp.float32).astype(jnp.bfloat16)
    key = jnp.dot(conv_out, w_key, preferred_element_type=jnp.float32).astype(jnp.bfloat16)
    value = jnp.dot(conv_out, w_value, preferred_element_type=jnp.float32).astype(jnp.bfloat16)
    head_size = w_query.shape[1]
    scale = 1.0 / math.sqrt(head_size)
    me = lax.axis_index("seq")
    query_pos = me * rows + jnp.arange(rows, dtype=jnp.int32)
    pairs = jnp.concatenate([key, value], axis=1)
    blocks, sources = gather_earlier(pairs, shards, me)
    keys = blocks[:, :, :head_size].reshape(-1, head_size)
    values = blocks[:, :, head_size:].reshape(-1, head_size)
    key_pos = (sources[:, None] * rows + jnp.arange(rows, dtype=jnp.int32)[None, :]).reshape(-1)
    score = jnp.einsum("qd,kd->qk", query, keys, preferred_element_type=jnp.float32) * scale
    allowed = key_pos[None, :] <= query_pos[:, None]
    masked = jnp.where(allowed, score, -1e30)
    peak = jnp.max(masked, axis=1)
    weight = jnp.where(allowed, jnp.exp(masked - peak[:, None]), 0.0)
    total = jnp.sum(weight, axis=1)
    summed = jnp.dot(weight.astype(jnp.bfloat16), values, preferred_element_type=jnp.float32)
    attended = (summed / total[:, None]).astype(jnp.bfloat16)
    return (conv_out, attended)


def solution(mesh):
    in_specs = (
        P(("groups", "seq"), None),
        P(("groups", "seq"), None),
        P(("groups", "seq"), None),
        P("seq", None),
        P(),
        P(),
        P(),
    )
    out_specs = (P(("groups", "seq"), None), P(("groups", "seq"), None))
    return jax.shard_map(
        on_device, mesh=mesh, in_specs=in_specs, out_specs=out_specs, check_vma=False
    )
```

```python
import math

import jax
import jax.numpy as jnp
from jax import lax
from jax.sharding import PartitionSpec as P

careful = lax.Precision.HIGH


def angle_table(rows, cols, period, sign):
    product = (
        lax.broadcasted_iota(jnp.int32, (rows, cols), 0)
        * lax.broadcasted_iota(jnp.int32, (rows, cols), 1)
        % period
    )
    phase = product.astype(jnp.float32) * (sign * 2.0 * math.pi / period)
    return (jnp.cos(phase), jnp.sin(phase))


def spectrum(signal):
    count, half, width = signal.shape
    outer = 2 * half
    whole = outer * width
    cos_a, sin_a = angle_table(outer, half, outer, -1.0)
    real_a = jnp.einsum(
        "kn,cnm->ckm", cos_a, signal, precision=careful, preferred_element_type=jnp.float32
    )
    imag_a = jnp.einsum(
        "kn,cnm->ckm", sin_a, signal, precision=careful, preferred_element_type=jnp.float32
    )
    cos_t, sin_t = angle_table(outer, width, whole, -1.0)
    real_b = real_a * cos_t - imag_a * sin_t
    imag_b = real_a * sin_t + imag_a * cos_t
    cos_c, sin_c = angle_table(width, width, width, -1.0)
    real_x = jnp.einsum("cqn,kn->cqk", real_b, cos_c, precision=careful) - jnp.einsum(
        "cqn,kn->cqk", imag_b, sin_c, precision=careful
    )
    imag_x = jnp.einsum("cqn,kn->cqk", real_b, sin_c, precision=careful) + jnp.einsum(
        "cqn,kn->cqk", imag_b, cos_c, precision=careful
    )
    return (real_x, imag_x)


def spectrum_pair(signal, taps):
    count, half, width = signal.shape
    outer = 2 * half
    whole = outer * width
    cos_a, sin_a = angle_table(outer, half, outer, -1.0)

    def stage(table, values):
        return jnp.einsum(
            "kn,cnm->ckm", table, values, precision=careful, preferred_element_type=jnp.float32
        )

    real_a = stage(cos_a, signal) - stage(sin_a, taps)
    imag_a = stage(sin_a, signal) + stage(cos_a, taps)
    cos_t, sin_t = angle_table(outer, width, whole, -1.0)
    real_b = real_a * cos_t - imag_a * sin_t
    imag_b = real_a * sin_t + imag_a * cos_t
    cos_c, sin_c = angle_table(width, width, width, -1.0)
    real_x = jnp.einsum("cqn,kn->cqk", real_b, cos_c, precision=careful) - jnp.einsum(
        "cqn,kn->cqk", imag_b, sin_c, precision=careful
    )
    imag_x = jnp.einsum("cqn,kn->cqk", real_b, sin_c, precision=careful) + jnp.einsum(
        "cqn,kn->cqk", imag_b, cos_c, precision=careful
    )
    return (real_x, imag_x)


def mirrored(values):
    head = jnp.roll(jnp.flip(values[:, :1, :], axis=2), 1, axis=2)
    rest = jnp.flip(values[:, 1:, :], axis=(1, 2))
    return jnp.concatenate([head, rest], axis=1)


def inverse_real(real_y, imag_y, half):
    count, outer, width = real_y.shape
    whole = outer * width
    cos_c, sin_c = angle_table(width, width, width, 1.0)
    real_c = jnp.einsum("cqk,kn->cqn", real_y, cos_c, precision=careful) - jnp.einsum(
        "cqk,kn->cqn", imag_y, sin_c, precision=careful
    )
    imag_c = jnp.einsum("cqk,kn->cqn", real_y, sin_c, precision=careful) + jnp.einsum(
        "cqk,kn->cqn", imag_y, cos_c, precision=careful
    )
    cos_t, sin_t = angle_table(outer, width, whole, 1.0)
    real_d = real_c * cos_t - imag_c * sin_t
    imag_d = real_c * sin_t + imag_c * cos_t
    cos_a, sin_a = angle_table(half, outer, outer, 1.0)
    result = jnp.einsum("nk,ckm->cnm", cos_a, real_d, precision=careful) - jnp.einsum(
        "nk,ckm->cnm", sin_a, imag_d, precision=careful
    )
    return (result / whole).reshape(count, half * width)


def make_convolver(width, pieces, waits=None):
    signal = pieces[0]
    taps = pieces[1]
    count = signal.shape[1]
    length = signal.shape[2]
    half = length // width
    real_z, imag_z = spectrum_pair(
        signal.reshape(count, half, width), taps.reshape(count, half, width)
    )
    real_r = mirrored(real_z)
    imag_r = mirrored(imag_z)
    prod_real = (real_z * imag_z + real_r * imag_r) * 0.5
    prod_imag = (imag_z * imag_z - imag_r * imag_r - real_z * real_z + real_r * real_r) * 0.25
    if waits is not None:
        prod_real, prod_imag, waits = lax.optimization_barrier((prod_real, prod_imag, waits))
    long_part = inverse_real(prod_real, prod_imag, half).reshape(1, count, length)
    return long_part, waits


def gather_earlier(block, shards, me):
    plane = 4 if shards % 4 == 0 else 1
    lines = shards // plane
    lane = me % plane
    level = me // plane
    stack = [block]
    for depth in range(1, lines):
        step = depth * plane
        stack.append(lax.ppermute(block, "seq", [(i, i + step) for i in range(shards - step)]))
    stack = jnp.stack(stack)
    src_level = level - jnp.arange(lines, dtype=jnp.int32)

    def origin(from_lane):
        return jnp.where(src_level >= 0, src_level * plane + from_lane, shards)

    if plane == 1:
        return stack, origin(lane)
    base = [p * plane for p in range(lines)]
    across = [(b + l, b + (l ^ 2)) for b in base for l in range(plane)]
    beside = [(b + l, b + (l ^ 1)) for b in base for l in range(plane)]
    far = lax.ppermute(stack, "seq", across)
    both = jnp.concatenate([stack, far])
    near = lax.ppermute(both, "seq", beside)
    blocks = jnp.concatenate([both, near])
    sources = jnp.concatenate(
        [origin(lane), origin(lane ^ 2), origin(lane ^ 1), origin(lane ^ 3)]
    )
    return blocks, sources

def on_device(left_stream, right_stream, gate_stream, filter_taps, w_query, w_key, w_value):
    rows, channels = left_stream.shape
    shards = lax.axis_size("seq")
    group = channels // shards
    mixed = (left_stream.astype(jnp.float32) * right_stream.astype(jnp.float32)).astype(
        jnp.bfloat16
    )
    mixed_groups = mixed.T.reshape(shards, group, rows)
    tap_groups = filter_taps.T.reshape(shards, group, rows)
    chunks = 2 if group % 16 == 0 else 1
    sub = group // chunks
    arrived = []
    for k in range(chunks):
        cut = slice(k * sub, (k + 1) * sub)
        payload = jnp.concatenate([mixed_groups[:, cut], tap_groups[:, cut]], axis=1)
        arrived.append(lax.all_to_all(payload, "seq", split_axis=0, concat_axis=2, tiled=True))
    pieces = []
    previous = None
    for k in range(chunks):
        got = arrived[k]
        back = None
        if previous is not None:
            got, previous = lax.optimization_barrier((got, previous))
            back = lax.all_to_all(previous, "seq", split_axis=0, concat_axis=0, tiled=True)
        long_k, back = make_convolver(rows, (got[:, :sub], got[:, sub : 2 * sub]), back)
        if back is not None:
            pieces.append(back)
        previous = long_k.reshape(sub, shards, rows).transpose(1, 0, 2)
    pieces.append(lax.all_to_all(previous, "seq", split_axis=0, concat_axis=0, tiled=True))
    returned = jnp.concatenate(pieces, axis=1)
    long_part = returned.reshape(channels, rows).T
    conv_out = (gate_stream.astype(jnp.float32) * long_part).astype(jnp.bfloat16)
    query = jnp.dot(conv_out, w_query, preferred_element_type=jnp.float32).astype(jnp.bfloat16)
    key = jnp.dot(conv_out, w_key, preferred_element_type=jnp.float32).astype(jnp.bfloat16)
    value = jnp.dot(conv_out, w_value, preferred_element_type=jnp.float32).astype(jnp.bfloat16)
    head_size = w_query.shape[1]
    scale = 1.0 / math.sqrt(head_size)
    me = lax.axis_index("seq")
    query_pos = me * rows + jnp.arange(rows, dtype=jnp.int32)
    pairs = jnp.concatenate([key, value], axis=1)
    blocks, sources = gather_earlier(pairs, shards, me)
    keys = blocks[:, :, :head_size].reshape(-1, head_size)
    values = blocks[:, :, head_size:].reshape(-1, head_size)
    key_pos = (sources[:, None] * rows + jnp.arange(rows, dtype=jnp.int32)[None, :]).reshape(-1)
    score = jnp.einsum("qd,kd->qk", query, keys, preferred_element_type=jnp.float32) * scale
    allowed = key_pos[None, :] <= query_pos[:, None]
    masked = jnp.where(allowed, score, -1e30)
    peak = jnp.max(masked, axis=1)
    weight = jnp.where(allowed, jnp.exp(masked - peak[:, None]), 0.0)
    total = jnp.sum(weight, axis=1)
    summed = jnp.dot(weight.astype(jnp.bfloat16), values, preferred_element_type=jnp.float32)
    attended = (summed / total[:, None]).astype(jnp.bfloat16)
    return (conv_out, attended)


def solution(mesh):
    in_specs = (
        P(("groups", "seq"), None),
        P(("groups", "seq"), None),
        P(("groups", "seq"), None),
        P("seq", None),
        P(),
        P(),
        P(),
    )
    out_specs = (P(("groups", "seq"), None), P(("groups", "seq"), None))
    return jax.shard_map(
        on_device, mesh=mesh, in_specs=in_specs, out_specs=out_specs, check_vma=False
    )
```

```python
import math

import jax
import jax.numpy as jnp
from jax import lax
from jax.sharding import PartitionSpec as P

careful = lax.Precision.HIGH


def angle_table(rows, cols, period, sign):
    product = (
        lax.broadcasted_iota(jnp.int32, (rows, cols), 0)
        * lax.broadcasted_iota(jnp.int32, (rows, cols), 1)
        % period
    )
    phase = product.astype(jnp.float32) * (sign * 2.0 * math.pi / period)
    return (jnp.cos(phase), jnp.sin(phase))


def spectrum(signal):
    count, half, width = signal.shape
    outer = 2 * half
    whole = outer * width
    cos_a, sin_a = angle_table(outer, half, outer, -1.0)
    both_a = jnp.einsum(
        "kn,cnm->ckm",
        jnp.concatenate([cos_a, sin_a]),
        signal,
        precision=careful,
        preferred_element_type=jnp.float32,
    )
    real_a = both_a[:, :outer]
    imag_a = both_a[:, outer:]
    cos_t, sin_t = angle_table(outer, width, whole, -1.0)
    real_b = real_a * cos_t - imag_a * sin_t
    imag_b = real_a * sin_t + imag_a * cos_t
    cos_c, sin_c = angle_table(width, width, width, -1.0)
    rotate = jnp.concatenate(
        [
            jnp.concatenate([cos_c.T, sin_c.T], axis=1),
            jnp.concatenate([-sin_c.T, cos_c.T], axis=1),
        ]
    )
    return jnp.einsum(
        "cqn,nk->cqk", jnp.concatenate([real_b, imag_b], axis=2), rotate, precision=careful
    )


def inverse_real(product, half):
    count, outer, double = product.shape
    width = double // 2
    whole = outer * width
    cos_c, sin_c = angle_table(width, width, width, 1.0)
    rotate = jnp.concatenate(
        [
            jnp.concatenate([cos_c.T, sin_c.T], axis=1),
            jnp.concatenate([-sin_c.T, cos_c.T], axis=1),
        ]
    )
    both_c = jnp.einsum("cqk,kn->cqn", product, rotate, precision=careful)
    real_c = both_c[:, :, :width]
    imag_c = both_c[:, :, width:]
    cos_t, sin_t = angle_table(outer, width, whole, 1.0)
    real_d = real_c * cos_t - imag_c * sin_t
    imag_d = real_c * sin_t + imag_c * cos_t
    cos_a, sin_a = angle_table(half, outer, outer, 1.0)
    result = jnp.einsum(
        "nk,ckm->cnm",
        jnp.concatenate([cos_a, -sin_a], axis=1),
        jnp.concatenate([real_d, imag_d], axis=1),
        precision=careful,
    )
    return (result / whole).reshape(count, half * width)


def make_convolver(width, pieces, waits=None):
    signal = pieces[0]
    taps = pieces[1]
    count = signal.shape[1]
    length = signal.shape[2]
    half = length // width
    spectra = spectrum(jnp.concatenate([signal[0], taps[0]]).reshape(2 * count, half, width))
    sig_real = spectra[:count, :, :width]
    sig_imag = spectra[:count, :, width:]
    tap_real = spectra[count:, :, :width]
    tap_imag = spectra[count:, :, width:]
    product = jnp.concatenate(
        [sig_real * tap_real - sig_imag * tap_imag, sig_real * tap_imag + sig_imag * tap_real],
        axis=2,
    )
    if waits is not None:
        product, waits = lax.optimization_barrier((product, waits))
    long_part = inverse_real(product, half).reshape(1, count, length)
    return long_part, waits


def gather_earlier(block, shards, me):
    plane = 4 if shards % 4 == 0 else 1
    lines = shards // plane
    lane = me % plane
    level = me // plane
    stack = [block]
    for depth in range(1, lines):
        step = depth * plane
        stack.append(lax.ppermute(block, "seq", [(i, i + step) for i in range(shards - step)]))
    stack = jnp.stack(stack)
    src_level = level - jnp.arange(lines, dtype=jnp.int32)

    def origin(from_lane):
        return jnp.where(src_level >= 0, src_level * plane + from_lane, shards)

    if plane == 1:
        return stack, origin(lane)
    base = [p * plane for p in range(lines)]
    across = [(b + l, b + (l ^ 2)) for b in base for l in range(plane)]
    beside = [(b + l, b + (l ^ 1)) for b in base for l in range(plane)]
    far = lax.ppermute(stack, "seq", across)
    both = jnp.concatenate([stack, far])
    near = lax.ppermute(both, "seq", beside)
    blocks = jnp.concatenate([both, near])
    sources = jnp.concatenate(
        [origin(lane), origin(lane ^ 2), origin(lane ^ 1), origin(lane ^ 3)]
    )
    return blocks, sources

def on_device(left_stream, right_stream, gate_stream, filter_taps, w_query, w_key, w_value):
    rows, channels = left_stream.shape
    shards = lax.axis_size("seq")
    group = channels // shards
    mixed = (left_stream.astype(jnp.float32) * right_stream.astype(jnp.float32)).astype(
        jnp.bfloat16
    )
    mixed_groups = mixed.T.reshape(shards, group, rows)
    tap_groups = filter_taps.T.reshape(shards, group, rows)
    chunks = 2 if group % 16 == 0 else 1
    sub = group // chunks
    arrived = []
    for k in range(chunks):
        cut = slice(k * sub, (k + 1) * sub)
        payload = jnp.concatenate([mixed_groups[:, cut], tap_groups[:, cut]], axis=1)
        arrived.append(lax.all_to_all(payload, "seq", split_axis=0, concat_axis=2, tiled=True))
    pieces = []
    previous = None
    for k in range(chunks):
        got = arrived[k]
        back = None
        if previous is not None:
            got, previous = lax.optimization_barrier((got, previous))
            back = lax.all_to_all(previous, "seq", split_axis=0, concat_axis=0, tiled=True)
        long_k, back = make_convolver(rows, (got[:, :sub], got[:, sub : 2 * sub]), back)
        if back is not None:
            pieces.append(back)
        previous = long_k.reshape(sub, shards, rows).transpose(1, 0, 2)
    pieces.append(lax.all_to_all(previous, "seq", split_axis=0, concat_axis=0, tiled=True))
    returned = jnp.concatenate(pieces, axis=1)
    long_part = returned.reshape(channels, rows).T
    conv_out = (gate_stream.astype(jnp.float32) * long_part).astype(jnp.bfloat16)
    query = jnp.dot(conv_out, w_query, preferred_element_type=jnp.float32).astype(jnp.bfloat16)
    key = jnp.dot(conv_out, w_key, preferred_element_type=jnp.float32).astype(jnp.bfloat16)
    value = jnp.dot(conv_out, w_value, preferred_element_type=jnp.float32).astype(jnp.bfloat16)
    head_size = w_query.shape[1]
    scale = 1.0 / math.sqrt(head_size)
    me = lax.axis_index("seq")
    query_pos = me * rows + jnp.arange(rows, dtype=jnp.int32)
    pairs = jnp.concatenate([key, value], axis=1)
    blocks, sources = gather_earlier(pairs, shards, me)
    keys = blocks[:, :, :head_size].reshape(-1, head_size)
    values = blocks[:, :, head_size:].reshape(-1, head_size)
    key_pos = (sources[:, None] * rows + jnp.arange(rows, dtype=jnp.int32)[None, :]).reshape(-1)
    score = jnp.einsum("qd,kd->qk", query, keys, preferred_element_type=jnp.float32) * scale
    allowed = key_pos[None, :] <= query_pos[:, None]
    masked = jnp.where(allowed, score, -1e30)
    peak = jnp.max(masked, axis=1)
    weight = jnp.where(allowed, jnp.exp(masked - peak[:, None]), 0.0)
    total = jnp.sum(weight, axis=1)
    summed = jnp.dot(weight.astype(jnp.bfloat16), values, preferred_element_type=jnp.float32)
    attended = (summed / total[:, None]).astype(jnp.bfloat16)
    return (conv_out, attended)


def solution(mesh):
    in_specs = (
        P(("groups", "seq"), None),
        P(("groups", "seq"), None),
        P(("groups", "seq"), None),
        P("seq", None),
        P(),
        P(),
        P(),
    )
    out_specs = (P(("groups", "seq"), None), P(("groups", "seq"), None))
    return jax.shard_map(
        on_device, mesh=mesh, in_specs=in_specs, out_specs=out_specs, check_vma=False
    )
```

```python
import math

import jax
import jax.numpy as jnp
from jax import lax
from jax.sharding import PartitionSpec as P

careful = lax.Precision.HIGH


def angle_table(rows, cols, period, sign):
    product = (
        lax.broadcasted_iota(jnp.int32, (rows, cols), 0)
        * lax.broadcasted_iota(jnp.int32, (rows, cols), 1)
        % period
    )
    phase = product.astype(jnp.float32) * (sign * 2.0 * math.pi / period)
    return (jnp.cos(phase), jnp.sin(phase))


def spectrum(signal):
    count, half, width = signal.shape
    outer = 2 * half
    whole = outer * width
    cos_a, sin_a = angle_table(outer, half, outer, -1.0)
    both_a = jnp.einsum(
        "kn,cnm->ckm",
        jnp.concatenate([cos_a, sin_a]),
        signal,
        precision=careful,
        preferred_element_type=jnp.float32,
    )
    real_a = both_a[:, :outer]
    imag_a = both_a[:, outer:]
    cos_t, sin_t = angle_table(outer, width, whole, -1.0)
    real_b = real_a * cos_t - imag_a * sin_t
    imag_b = real_a * sin_t + imag_a * cos_t
    cos_c, sin_c = angle_table(width, width, width, -1.0)
    rotate = jnp.concatenate(
        [
            jnp.concatenate([cos_c.T, sin_c.T], axis=1),
            jnp.concatenate([-sin_c.T, cos_c.T], axis=1),
        ]
    )
    return jnp.einsum(
        "cqn,nk->cqk", jnp.concatenate([real_b, imag_b], axis=2), rotate, precision=careful
    )


def inverse_real(product, half):
    count, outer, double = product.shape
    width = double // 2
    whole = outer * width
    cos_c, sin_c = angle_table(width, width, width, 1.0)
    rotate = jnp.concatenate(
        [
            jnp.concatenate([cos_c.T, sin_c.T], axis=1),
            jnp.concatenate([-sin_c.T, cos_c.T], axis=1),
        ]
    )
    both_c = jnp.einsum("cqk,kn->cqn", product, rotate, precision=careful)
    real_c = both_c[:, :, :width]
    imag_c = both_c[:, :, width:]
    cos_t, sin_t = angle_table(outer, width, whole, 1.0)
    real_d = real_c * cos_t - imag_c * sin_t
    imag_d = real_c * sin_t + imag_c * cos_t
    cos_a, sin_a = angle_table(half, outer, outer, 1.0)
    result = jnp.einsum(
        "nk,ckm->cnm",
        jnp.concatenate([cos_a, -sin_a], axis=1),
        jnp.concatenate([real_d, imag_d], axis=1),
        precision=careful,
    )
    return (result / whole).reshape(count, half * width)


def make_convolver(width, pieces, waits=None):
    signal = pieces[0]
    taps = pieces[1]
    count = signal.shape[1]
    length = signal.shape[2]
    half = length // width
    spectra = spectrum(jnp.concatenate([signal[0], taps[0]]).reshape(2 * count, half, width))
    sig_real = spectra[:count, :, :width]
    sig_imag = spectra[:count, :, width:]
    tap_real = spectra[count:, :, :width]
    tap_imag = spectra[count:, :, width:]
    product = jnp.concatenate(
        [sig_real * tap_real - sig_imag * tap_imag, sig_real * tap_imag + sig_imag * tap_real],
        axis=2,
    )
    long_part = inverse_real(product, half).reshape(1, count, length)
    if waits is not None:
        long_part, waits = lax.optimization_barrier((long_part, waits))
    return long_part, waits


def gather_earlier(block, shards, me):
    plane = 4 if shards % 4 == 0 else 1
    lines = shards // plane
    lane = me % plane
    level = me // plane
    stack = [block]
    for depth in range(1, lines):
        step = depth * plane
        stack.append(lax.ppermute(block, "seq", [(i, i + step) for i in range(shards - step)]))
    stack = jnp.stack(stack)
    src_level = level - jnp.arange(lines, dtype=jnp.int32)

    def origin(from_lane):
        return jnp.where(src_level >= 0, src_level * plane + from_lane, shards)

    if plane == 1:
        return stack, origin(lane)
    base = [p * plane for p in range(lines)]
    across = [(b + l, b + (l ^ 2)) for b in base for l in range(plane)]
    beside = [(b + l, b + (l ^ 1)) for b in base for l in range(plane)]
    far = lax.ppermute(stack, "seq", across)
    both = jnp.concatenate([stack, far])
    near = lax.ppermute(both, "seq", beside)
    blocks = jnp.concatenate([both, near])
    sources = jnp.concatenate(
        [origin(lane), origin(lane ^ 2), origin(lane ^ 1), origin(lane ^ 3)]
    )
    return blocks, sources

def on_device(left_stream, right_stream, gate_stream, filter_taps, w_query, w_key, w_value):
    rows, channels = left_stream.shape
    shards = lax.axis_size("seq")
    group = channels // shards
    mixed = (left_stream.astype(jnp.float32) * right_stream.astype(jnp.float32)).astype(
        jnp.bfloat16
    )
    chunks = 2 if group % 16 == 0 else 1
    sub = group // chunks
    mixed_groups = mixed.reshape(rows, shards, chunks, sub)
    tap_groups = filter_taps.reshape(rows, shards, chunks, sub)
    arrived = []
    for k in range(chunks):
        payload = jnp.concatenate(
            [mixed_groups[:, :, k].transpose(1, 2, 0), tap_groups[:, :, k].transpose(1, 2, 0)],
            axis=1,
        )
        arrived.append(lax.all_to_all(payload, "seq", split_axis=0, concat_axis=2, tiled=True))
    pieces = []
    previous = None
    for k in range(chunks):
        got = arrived[k]
        back = None
        if previous is not None:
            got, previous = lax.optimization_barrier((got, previous))
            back = lax.all_to_all(previous, "seq", split_axis=0, concat_axis=0, tiled=True)
        long_k, back = make_convolver(rows, (got[:, :sub], got[:, sub : 2 * sub]), back)
        if back is not None:
            pieces.append(back)
        previous = long_k.reshape(sub, shards, rows).transpose(1, 0, 2)
    pieces.append(lax.all_to_all(previous, "seq", split_axis=0, concat_axis=0, tiled=True))
    returned = jnp.concatenate(pieces, axis=1)
    long_part = returned.reshape(channels, rows).T
    conv_out = (gate_stream.astype(jnp.float32) * long_part).astype(jnp.bfloat16)
    query = jnp.dot(conv_out, w_query, preferred_element_type=jnp.float32).astype(jnp.bfloat16)
    key = jnp.dot(conv_out, w_key, preferred_element_type=jnp.float32).astype(jnp.bfloat16)
    value = jnp.dot(conv_out, w_value, preferred_element_type=jnp.float32).astype(jnp.bfloat16)
    head_size = w_query.shape[1]
    scale = 1.0 / math.sqrt(head_size)
    me = lax.axis_index("seq")
    query_pos = me * rows + jnp.arange(rows, dtype=jnp.int32)
    pairs = jnp.concatenate([key, value], axis=1)
    blocks, sources = gather_earlier(pairs, shards, me)
    keys = blocks[:, :, :head_size].reshape(-1, head_size)
    values = blocks[:, :, head_size:].reshape(-1, head_size)
    key_pos = (sources[:, None] * rows + jnp.arange(rows, dtype=jnp.int32)[None, :]).reshape(-1)
    score = jnp.einsum("qd,kd->qk", query, keys, preferred_element_type=jnp.float32) * scale
    allowed = key_pos[None, :] <= query_pos[:, None]
    masked = jnp.where(allowed, score, -1e30)
    peak = jnp.max(masked, axis=1)
    weight = jnp.where(allowed, jnp.exp(masked - peak[:, None]), 0.0)
    total = jnp.sum(weight, axis=1)
    summed = jnp.dot(weight.astype(jnp.bfloat16), values, preferred_element_type=jnp.float32)
    attended = (summed / total[:, None]).astype(jnp.bfloat16)
    return (conv_out, attended)


def solution(mesh):
    in_specs = (
        P(("groups", "seq"), None),
        P(("groups", "seq"), None),
        P(("groups", "seq"), None),
        P("seq", None),
        P(),
        P(),
        P(),
    )
    out_specs = (P(("groups", "seq"), None), P(("groups", "seq"), None))
    return jax.shard_map(
        on_device, mesh=mesh, in_specs=in_specs, out_specs=out_specs, check_vma=False
    )
```

```python
import math

import jax
import jax.numpy as jnp
from jax import lax
from jax.sharding import PartitionSpec as P

careful = lax.Precision.HIGH


def angle_table(rows, cols, period, sign):
    product = (
        lax.broadcasted_iota(jnp.int32, (rows, cols), 0)
        * lax.broadcasted_iota(jnp.int32, (rows, cols), 1)
        % period
    )
    phase = product.astype(jnp.float32) * (sign * 2.0 * math.pi / period)
    return (jnp.cos(phase), jnp.sin(phase))


def rotation(width, sign):
    cos_c, sin_c = angle_table(width, width, width, sign)
    return jnp.concatenate(
        [jnp.concatenate([cos_c, -sin_c], axis=1), jnp.concatenate([sin_c, cos_c], axis=1)]
    )


def convolve_columns(both, half, waits=None):
    length, double = both.shape
    count = double // 2
    width = length // half
    outer = 2 * half
    whole = outer * width
    values = both.reshape(half, width, double)
    cos_a, sin_a = angle_table(outer, half, outer, -1.0)
    stage_a = jnp.einsum(
        "kd,drc->krc",
        jnp.concatenate([cos_a, sin_a]),
        values,
        precision=careful,
        preferred_element_type=jnp.float32,
    )
    real_a = stage_a[:outer]
    imag_a = stage_a[outer:]
    cos_t, sin_t = angle_table(outer, width, whole, -1.0)
    cos_t = cos_t[:, :, None]
    sin_t = sin_t[:, :, None]
    turned = jnp.concatenate(
        [real_a * cos_t - imag_a * sin_t, real_a * sin_t + imag_a * cos_t], axis=1
    )
    spectra = jnp.einsum("kr,qrc->qkc", rotation(width, -1.0), turned, precision=careful)
    sig_real = spectra[:, :width, :count]
    sig_imag = spectra[:, width:, :count]
    tap_real = spectra[:, :width, count:]
    tap_imag = spectra[:, width:, count:]
    product = jnp.concatenate(
        [sig_real * tap_real - sig_imag * tap_imag, sig_real * tap_imag + sig_imag * tap_real],
        axis=1,
    )
    if waits is not None:
        product, waits = lax.optimization_barrier((product, waits))
    back_c = jnp.einsum("rk,qkc->qrc", rotation(width, 1.0), product, precision=careful)
    real_c = back_c[:, :width]
    imag_c = back_c[:, width:]
    cos_t, sin_t = angle_table(outer, width, whole, 1.0)
    cos_t = cos_t[:, :, None]
    sin_t = sin_t[:, :, None]
    unturned = jnp.concatenate(
        [real_c * cos_t - imag_c * sin_t, real_c * sin_t + imag_c * cos_t], axis=0
    )
    cos_a, sin_a = angle_table(half, outer, outer, 1.0)
    result = jnp.einsum(
        "dk,krc->drc", jnp.concatenate([cos_a, -sin_a], axis=1), unturned, precision=careful
    )
    return result / whole, waits


def gather_earlier(block, shards, me):
    plane = 4 if shards % 4 == 0 else 1
    lines = shards // plane
    lane = me % plane
    level = me // plane
    stack = [block]
    for depth in range(1, lines):
        step = depth * plane
        stack.append(lax.ppermute(block, "seq", [(i, i + step) for i in range(shards - step)]))
    stack = jnp.stack(stack)
    src_level = level - jnp.arange(lines, dtype=jnp.int32)

    def origin(from_lane):
        return jnp.where(src_level >= 0, src_level * plane + from_lane, shards)

    if plane == 1:
        return stack, origin(lane)
    base = [p * plane for p in range(lines)]
    across = [(b + l, b + (l ^ 2)) for b in base for l in range(plane)]
    beside = [(b + l, b + (l ^ 1)) for b in base for l in range(plane)]
    far = lax.ppermute(stack, "seq", across)
    both = jnp.concatenate([stack, far])
    near = lax.ppermute(both, "seq", beside)
    blocks = jnp.concatenate([both, near])
    sources = jnp.concatenate(
        [origin(lane), origin(lane ^ 2), origin(lane ^ 1), origin(lane ^ 3)]
    )
    return blocks, sources

def on_device(left_stream, right_stream, gate_stream, filter_taps, w_query, w_key, w_value):
    rows, channels = left_stream.shape
    shards = lax.axis_size("seq")
    group = channels // shards
    mixed = (left_stream.astype(jnp.float32) * right_stream.astype(jnp.float32)).astype(
        jnp.bfloat16
    )
    mixed_groups = mixed.T.reshape(shards, group, rows)
    tap_groups = filter_taps.T.reshape(shards, group, rows)
    chunks = 2 if group % 16 == 0 else 1
    sub = group // chunks
    half = shards
    mixed_groups = mixed.reshape(rows, shards, chunks, sub)
    tap_groups = filter_taps.reshape(rows, shards, chunks, sub)
    arrived = []
    for k in range(chunks):
        payload = jnp.concatenate([mixed_groups[:, :, k], tap_groups[:, :, k]], axis=2)
        got = lax.all_to_all(payload, "seq", split_axis=1, concat_axis=0, tiled=True)
        arrived.append(got.reshape(shards * rows, 2 * sub))
    pieces = []
    previous = None
    for k in range(chunks):
        got = arrived[k]
        back = None
        if previous is not None:
            got, previous = lax.optimization_barrier((got, previous))
            back = lax.all_to_all(previous, "seq", split_axis=0, concat_axis=2, tiled=True)
        long_k, back = convolve_columns(got, half, back)
        if back is not None:
            pieces.append(back)
        previous = long_k.reshape(shards, rows, 1, sub)
    pieces.append(lax.all_to_all(previous, "seq", split_axis=0, concat_axis=2, tiled=True))
    returned = jnp.stack([piece.reshape(rows, shards, sub) for piece in pieces], axis=2)
    long_part = returned.reshape(rows, channels)

    conv_out = (gate_stream.astype(jnp.float32) * long_part).astype(jnp.bfloat16)
    query = jnp.dot(conv_out, w_query, preferred_element_type=jnp.float32).astype(jnp.bfloat16)
    key = jnp.dot(conv_out, w_key, preferred_element_type=jnp.float32).astype(jnp.bfloat16)
    value = jnp.dot(conv_out, w_value, preferred_element_type=jnp.float32).astype(jnp.bfloat16)
    head_size = w_query.shape[1]
    scale = 1.0 / math.sqrt(head_size)
    me = lax.axis_index("seq")
    query_pos = me * rows + jnp.arange(rows, dtype=jnp.int32)
    pairs = jnp.concatenate([key, value], axis=1)
    blocks, sources = gather_earlier(pairs, shards, me)
    keys = blocks[:, :, :head_size].reshape(-1, head_size)
    values = blocks[:, :, head_size:].reshape(-1, head_size)
    key_pos = (sources[:, None] * rows + jnp.arange(rows, dtype=jnp.int32)[None, :]).reshape(-1)
    score = jnp.einsum("qd,kd->qk", query, keys, preferred_element_type=jnp.float32) * scale
    allowed = key_pos[None, :] <= query_pos[:, None]
    masked = jnp.where(allowed, score, -1e30)
    peak = jnp.max(masked, axis=1)
    weight = jnp.where(allowed, jnp.exp(masked - peak[:, None]), 0.0)
    total = jnp.sum(weight, axis=1)
    summed = jnp.dot(weight.astype(jnp.bfloat16), values, preferred_element_type=jnp.float32)
    attended = (summed / total[:, None]).astype(jnp.bfloat16)
    return (conv_out, attended)


def solution(mesh):
    in_specs = (
        P(("groups", "seq"), None),
        P(("groups", "seq"), None),
        P(("groups", "seq"), None),
        P("seq", None),
        P(),
        P(),
        P(),
    )
    out_specs = (P(("groups", "seq"), None), P(("groups", "seq"), None))
    return jax.shard_map(
        on_device, mesh=mesh, in_specs=in_specs, out_specs=out_specs, check_vma=False
    )
```

```python
import math

import jax
import jax.numpy as jnp
from jax import lax
from jax.sharding import PartitionSpec as P

careful = lax.Precision.HIGH


def angle_table(rows, cols, period, sign):
    product = (
        lax.broadcasted_iota(jnp.int32, (rows, cols), 0)
        * lax.broadcasted_iota(jnp.int32, (rows, cols), 1)
        % period
    )
    phase = product.astype(jnp.float32) * (sign * 2.0 * math.pi / period)
    return (jnp.cos(phase), jnp.sin(phase))


def spectrum(signal):
    half, count, width = signal.shape
    outer = 2 * half
    whole = outer * width
    cos_a, sin_a = angle_table(outer, half, outer, -1.0)
    both_a = jnp.einsum(
        "kn,ncm->ckm",
        jnp.concatenate([cos_a, sin_a]),
        signal,
        precision=careful,
        preferred_element_type=jnp.float32,
    )
    real_a = both_a[:, :outer]
    imag_a = both_a[:, outer:]
    cos_t, sin_t = angle_table(outer, width, whole, -1.0)
    real_b = real_a * cos_t - imag_a * sin_t
    imag_b = real_a * sin_t + imag_a * cos_t
    cos_c, sin_c = angle_table(width, width, width, -1.0)
    rotate = jnp.concatenate(
        [
            jnp.concatenate([cos_c.T, sin_c.T], axis=1),
            jnp.concatenate([-sin_c.T, cos_c.T], axis=1),
        ]
    )
    return jnp.einsum(
        "cqn,nk->cqk", jnp.concatenate([real_b, imag_b], axis=2), rotate, precision=careful
    )


def inverse_real(product, half):
    count, outer, double = product.shape
    width = double // 2
    whole = outer * width
    cos_c, sin_c = angle_table(width, width, width, 1.0)
    rotate = jnp.concatenate(
        [
            jnp.concatenate([cos_c.T, sin_c.T], axis=1),
            jnp.concatenate([-sin_c.T, cos_c.T], axis=1),
        ]
    )
    both_c = jnp.einsum("cqk,kn->cqn", product, rotate, precision=careful)
    real_c = both_c[:, :, :width]
    imag_c = both_c[:, :, width:]
    cos_t, sin_t = angle_table(outer, width, whole, 1.0)
    real_d = real_c * cos_t - imag_c * sin_t
    imag_d = real_c * sin_t + imag_c * cos_t
    cos_a, sin_a = angle_table(half, outer, outer, 1.0)
    result = jnp.einsum(
        "nk,ckm->cnm",
        jnp.concatenate([cos_a, -sin_a], axis=1),
        jnp.concatenate([real_d, imag_d], axis=1),
        precision=careful,
    )
    return (result / whole).reshape(count, half * width)


def make_convolver(both, waits=None):
    half, double, width = both.shape
    count = double // 2
    length = half * width
    spectra = spectrum(both)
    sig_real = spectra[:count, :, :width]
    sig_imag = spectra[:count, :, width:]
    tap_real = spectra[count:, :, :width]
    tap_imag = spectra[count:, :, width:]
    product = jnp.concatenate(
        [sig_real * tap_real - sig_imag * tap_imag, sig_real * tap_imag + sig_imag * tap_real],
        axis=2,
    )
    if waits is not None:
        product, waits = lax.optimization_barrier((product, waits))
    long_part = inverse_real(product, half).reshape(1, count, length)
    return long_part, waits


def gather_earlier(block, shards, me):
    plane = 4 if shards % 4 == 0 else 1
    lines = shards // plane
    lane = me % plane
    level = me // plane
    stack = [block]
    for depth in range(1, lines):
        step = depth * plane
        stack.append(lax.ppermute(block, "seq", [(i, i + step) for i in range(shards - step)]))
    stack = jnp.stack(stack)
    src_level = level - jnp.arange(lines, dtype=jnp.int32)

    def origin(from_lane):
        return jnp.where(src_level >= 0, src_level * plane + from_lane, shards)

    if plane == 1:
        return stack, origin(lane)
    base = [p * plane for p in range(lines)]
    across = [(b + l, b + (l ^ 2)) for b in base for l in range(plane)]
    beside = [(b + l, b + (l ^ 1)) for b in base for l in range(plane)]
    far = lax.ppermute(stack, "seq", across)
    both = jnp.concatenate([stack, far])
    near = lax.ppermute(both, "seq", beside)
    blocks = jnp.concatenate([both, near])
    sources = jnp.concatenate(
        [origin(lane), origin(lane ^ 2), origin(lane ^ 1), origin(lane ^ 3)]
    )
    return blocks, sources

def on_device(left_stream, right_stream, gate_stream, filter_taps, w_query, w_key, w_value):
    rows, channels = left_stream.shape
    shards = lax.axis_size("seq")
    group = channels // shards
    mixed = (left_stream.astype(jnp.float32) * right_stream.astype(jnp.float32)).astype(
        jnp.bfloat16
    )
    mixed_groups = mixed.T.reshape(shards, group, rows)
    tap_groups = filter_taps.T.reshape(shards, group, rows)
    chunks = 2 if group % 16 == 0 else 1
    sub = group // chunks
    arrived = []
    for k in range(chunks):
        cut = slice(k * sub, (k + 1) * sub)
        payload = jnp.concatenate([mixed_groups[:, cut], tap_groups[:, cut]], axis=1)
        arrived.append(lax.all_to_all(payload, "seq", split_axis=0, concat_axis=0, tiled=True))
    pieces = []
    previous = None
    for k in range(chunks):
        got = arrived[k]
        back = None
        if previous is not None:
            got, previous = lax.optimization_barrier((got, previous))
            back = lax.all_to_all(previous, "seq", split_axis=0, concat_axis=0, tiled=True)
        long_k, back = make_convolver(got, back)
        if back is not None:
            pieces.append(back)
        previous = long_k.reshape(sub, shards, rows).transpose(1, 0, 2)
    pieces.append(lax.all_to_all(previous, "seq", split_axis=0, concat_axis=0, tiled=True))
    returned = jnp.concatenate(pieces, axis=1)
    long_part = returned.reshape(channels, rows).T
    conv_out = (gate_stream.astype(jnp.float32) * long_part).astype(jnp.bfloat16)
    query = jnp.dot(conv_out, w_query, preferred_element_type=jnp.float32).astype(jnp.bfloat16)
    key = jnp.dot(conv_out, w_key, preferred_element_type=jnp.float32).astype(jnp.bfloat16)
    value = jnp.dot(conv_out, w_value, preferred_element_type=jnp.float32).astype(jnp.bfloat16)
    head_size = w_query.shape[1]
    scale = 1.0 / math.sqrt(head_size)
    me = lax.axis_index("seq")
    query_pos = me * rows + jnp.arange(rows, dtype=jnp.int32)
    pairs = jnp.concatenate([key, value], axis=1)
    blocks, sources = gather_earlier(pairs, shards, me)
    keys = blocks[:, :, :head_size].reshape(-1, head_size)
    values = blocks[:, :, head_size:].reshape(-1, head_size)
    key_pos = (sources[:, None] * rows + jnp.arange(rows, dtype=jnp.int32)[None, :]).reshape(-1)
    score = jnp.einsum("qd,kd->qk", query, keys, preferred_element_type=jnp.float32) * scale
    allowed = key_pos[None, :] <= query_pos[:, None]
    masked = jnp.where(allowed, score, -1e30)
    peak = jnp.max(masked, axis=1)
    weight = jnp.where(allowed, jnp.exp(masked - peak[:, None]), 0.0)
    total = jnp.sum(weight, axis=1)
    summed = jnp.dot(weight.astype(jnp.bfloat16), values, preferred_element_type=jnp.float32)
    attended = (summed / total[:, None]).astype(jnp.bfloat16)
    return (conv_out, attended)


def solution(mesh):
    in_specs = (
        P(("groups", "seq"), None),
        P(("groups", "seq"), None),
        P(("groups", "seq"), None),
        P("seq", None),
        P(),
        P(),
        P(),
    )
    out_specs = (P(("groups", "seq"), None), P(("groups", "seq"), None))
    return jax.shard_map(
        on_device, mesh=mesh, in_specs=in_specs, out_specs=out_specs, check_vma=False
    )
```

```python
import math

import jax
import jax.numpy as jnp
from jax import lax
from jax.sharding import PartitionSpec as P

careful = lax.Precision.HIGH


def angle_table(rows, cols, period, sign):
    product = (
        lax.broadcasted_iota(jnp.int32, (rows, cols), 0)
        * lax.broadcasted_iota(jnp.int32, (rows, cols), 1)
        % period
    )
    phase = product.astype(jnp.float32) * (sign * 2.0 * math.pi / period)
    return (jnp.cos(phase), jnp.sin(phase))


def spectrum(signal):
    half, count, width = signal.shape
    outer = 2 * half
    whole = outer * width
    cos_a, sin_a = angle_table(outer, half, outer, -1.0)
    both_a = jnp.einsum(
        "kn,ncm->ckm",
        jnp.concatenate([cos_a, sin_a]),
        signal,
        precision=careful,
        preferred_element_type=jnp.float32,
    )
    real_a = both_a[:, :outer]
    imag_a = both_a[:, outer:]
    cos_t, sin_t = angle_table(outer, width, whole, -1.0)
    real_b = real_a * cos_t - imag_a * sin_t
    imag_b = real_a * sin_t + imag_a * cos_t
    cos_c, sin_c = angle_table(width, width, width, -1.0)
    rotate = jnp.concatenate(
        [
            jnp.concatenate([cos_c.T, sin_c.T], axis=1),
            jnp.concatenate([-sin_c.T, cos_c.T], axis=1),
        ]
    )
    return jnp.einsum(
        "cqn,nk->cqk", jnp.concatenate([real_b, imag_b], axis=2), rotate, precision=careful
    )


def inverse_real(product, half, waits=None):
    count, outer, double = product.shape
    width = double // 2
    whole = outer * width
    cos_c, sin_c = angle_table(width, width, width, 1.0)
    rotate = jnp.concatenate(
        [
            jnp.concatenate([cos_c.T, sin_c.T], axis=1),
            jnp.concatenate([-sin_c.T, cos_c.T], axis=1),
        ]
    )
    both_c = jnp.einsum("cqk,kn->cqn", product, rotate, precision=careful)
    if waits is not None:
        both_c, waits = lax.optimization_barrier((both_c, waits))
    real_c = both_c[:, :, :width]
    imag_c = both_c[:, :, width:]
    cos_t, sin_t = angle_table(outer, width, whole, 1.0)
    real_d = real_c * cos_t - imag_c * sin_t
    imag_d = real_c * sin_t + imag_c * cos_t
    cos_a, sin_a = angle_table(half, outer, outer, 1.0)
    result = jnp.einsum(
        "nk,ckm->cnm",
        jnp.concatenate([cos_a, -sin_a], axis=1),
        jnp.concatenate([real_d, imag_d], axis=1),
        precision=careful,
    )
    return (result / whole).reshape(count, half * width), waits


def make_convolver(both, waits=None):
    half, double, width = both.shape
    count = double // 2
    length = half * width
    spectra = spectrum(both)
    sig_real = spectra[:count, :, :width]
    sig_imag = spectra[:count, :, width:]
    tap_real = spectra[count:, :, :width]
    tap_imag = spectra[count:, :, width:]
    product = jnp.concatenate(
        [sig_real * tap_real - sig_imag * tap_imag, sig_real * tap_imag + sig_imag * tap_real],
        axis=2,
    )
    long_part, waits = inverse_real(product, half, waits)
    long_part = long_part.reshape(1, count, length)
    return long_part, waits


def gather_earlier(block, shards, me):
    plane = 4 if shards % 4 == 0 else 1
    lines = shards // plane
    lane = me % plane
    level = me // plane
    stack = [block]
    for depth in range(1, lines):
        step = depth * plane
        stack.append(lax.ppermute(block, "seq", [(i, i + step) for i in range(shards - step)]))
    stack = jnp.stack(stack)
    src_level = level - jnp.arange(lines, dtype=jnp.int32)

    def origin(from_lane):
        return jnp.where(src_level >= 0, src_level * plane + from_lane, shards)

    if plane == 1:
        return stack, origin(lane)
    base = [p * plane for p in range(lines)]
    across = [(b + l, b + (l ^ 2)) for b in base for l in range(plane)]
    beside = [(b + l, b + (l ^ 1)) for b in base for l in range(plane)]
    far = lax.ppermute(stack, "seq", across)
    both = jnp.concatenate([stack, far])
    near = lax.ppermute(both, "seq", beside)
    blocks = jnp.concatenate([both, near])
    sources = jnp.concatenate(
        [origin(lane), origin(lane ^ 2), origin(lane ^ 1), origin(lane ^ 3)]
    )
    return blocks, sources

def on_device(left_stream, right_stream, gate_stream, filter_taps, w_query, w_key, w_value):
    rows, channels = left_stream.shape
    shards = lax.axis_size("seq")
    group = channels // shards
    mixed = (left_stream.astype(jnp.float32) * right_stream.astype(jnp.float32)).astype(
        jnp.bfloat16
    )
    mixed_groups = mixed.T.reshape(shards, group, rows)
    tap_groups = filter_taps.T.reshape(shards, group, rows)
    chunks = 2 if group % 16 == 0 else 1
    sub = group // chunks
    arrived = []
    for k in range(chunks):
        cut = slice(k * sub, (k + 1) * sub)
        payload = jnp.concatenate([mixed_groups[:, cut], tap_groups[:, cut]], axis=1)
        arrived.append(lax.all_to_all(payload, "seq", split_axis=0, concat_axis=0, tiled=True))
    pieces = []
    previous = None
    for k in range(chunks):
        got = arrived[k]
        back = None
        if previous is not None:
            got, previous = lax.optimization_barrier((got, previous))
            back = lax.all_to_all(previous, "seq", split_axis=0, concat_axis=0, tiled=True)
        long_k, back = make_convolver(got, back)
        if back is not None:
            pieces.append(back)
        previous = long_k.reshape(sub, shards, rows).transpose(1, 0, 2)
    pieces.append(lax.all_to_all(previous, "seq", split_axis=0, concat_axis=0, tiled=True))
    returned = jnp.concatenate(pieces, axis=1)
    long_part = returned.reshape(channels, rows).T
    conv_out = (gate_stream.astype(jnp.float32) * long_part).astype(jnp.bfloat16)
    query = jnp.dot(conv_out, w_query, preferred_element_type=jnp.float32).astype(jnp.bfloat16)
    key = jnp.dot(conv_out, w_key, preferred_element_type=jnp.float32).astype(jnp.bfloat16)
    value = jnp.dot(conv_out, w_value, preferred_element_type=jnp.float32).astype(jnp.bfloat16)
    head_size = w_query.shape[1]
    scale = 1.0 / math.sqrt(head_size)
    me = lax.axis_index("seq")
    query_pos = me * rows + jnp.arange(rows, dtype=jnp.int32)
    pairs = jnp.concatenate([key, value], axis=1)
    blocks, sources = gather_earlier(pairs, shards, me)
    keys = blocks[:, :, :head_size].reshape(-1, head_size)
    values = blocks[:, :, head_size:].reshape(-1, head_size)
    key_pos = (sources[:, None] * rows + jnp.arange(rows, dtype=jnp.int32)[None, :]).reshape(-1)
    score = jnp.einsum("qd,kd->qk", query, keys, preferred_element_type=jnp.float32) * scale
    allowed = key_pos[None, :] <= query_pos[:, None]
    masked = jnp.where(allowed, score, -1e30)
    peak = jnp.max(masked, axis=1)
    weight = jnp.where(allowed, jnp.exp(masked - peak[:, None]), 0.0)
    total = jnp.sum(weight, axis=1)
    summed = jnp.dot(weight.astype(jnp.bfloat16), values, preferred_element_type=jnp.float32)
    attended = (summed / total[:, None]).astype(jnp.bfloat16)
    return (conv_out, attended)


def solution(mesh):
    in_specs = (
        P(("groups", "seq"), None),
        P(("groups", "seq"), None),
        P(("groups", "seq"), None),
        P("seq", None),
        P(),
        P(),
        P(),
    )
    out_specs = (P(("groups", "seq"), None), P(("groups", "seq"), None))
    return jax.shard_map(
        on_device, mesh=mesh, in_specs=in_specs, out_specs=out_specs, check_vma=False
    )
```

```python
import math

import jax
import jax.numpy as jnp
from jax import lax
from jax.sharding import PartitionSpec as P

careful = lax.Precision.HIGH


def angle_table(rows, cols, period, sign):
    product = (
        lax.broadcasted_iota(jnp.int32, (rows, cols), 0)
        * lax.broadcasted_iota(jnp.int32, (rows, cols), 1)
        % period
    )
    phase = product.astype(jnp.float32) * (sign * 2.0 * math.pi / period)
    return (jnp.cos(phase), jnp.sin(phase))


def spectrum(signal):
    half, count, width = signal.shape
    outer = 2 * half
    whole = outer * width
    cos_a, sin_a = angle_table(outer, half, outer, -1.0)
    both_a = jnp.einsum(
        "kn,ncm->ckm",
        jnp.concatenate([cos_a, sin_a]),
        signal,
        precision=careful,
        preferred_element_type=jnp.float32,
    )
    real_a = both_a[:, :outer]
    imag_a = both_a[:, outer:]
    cos_t, sin_t = angle_table(outer, width, whole, -1.0)
    real_b = real_a * cos_t - imag_a * sin_t
    imag_b = real_a * sin_t + imag_a * cos_t
    cos_c, sin_c = angle_table(width, width, width, -1.0)
    rotate = jnp.concatenate(
        [
            jnp.concatenate([cos_c.T, sin_c.T], axis=1),
            jnp.concatenate([-sin_c.T, cos_c.T], axis=1),
        ]
    )
    return jnp.einsum(
        "cqn,nk->cqk", jnp.concatenate([real_b, imag_b], axis=2), rotate, precision=careful
    )


def inverse_real(product, half, waits=None):
    count, outer, double = product.shape
    width = double // 2
    whole = outer * width
    cos_c, sin_c = angle_table(width, width, width, 1.0)
    rotate = jnp.concatenate(
        [
            jnp.concatenate([cos_c.T, sin_c.T], axis=1),
            jnp.concatenate([-sin_c.T, cos_c.T], axis=1),
        ]
    )
    both_c = jnp.einsum("cqk,kn->cqn", product, rotate, precision=careful)
    if waits is not None:
        both_c, waits = lax.optimization_barrier((both_c, waits))
    real_c = both_c[:, :, :width]
    imag_c = both_c[:, :, width:]
    cos_t, sin_t = angle_table(outer, width, whole, 1.0)
    real_d = real_c * cos_t - imag_c * sin_t
    imag_d = real_c * sin_t + imag_c * cos_t
    cos_a, sin_a = angle_table(half, outer, outer, 1.0)
    result = jnp.einsum(
        "nk,ckm->cnm",
        jnp.concatenate([cos_a, -sin_a], axis=1),
        jnp.concatenate([real_d, imag_d], axis=1),
        precision=careful,
    )
    return (result / whole).reshape(count, half * width), waits


def make_convolver(both, waits=None):
    half, double, width = both.shape
    count = double // 2
    length = half * width
    spectra = spectrum(both)
    sig_real = spectra[:count, :, :width]
    sig_imag = spectra[:count, :, width:]
    tap_real = spectra[count:, :, :width]
    tap_imag = spectra[count:, :, width:]
    product = jnp.concatenate(
        [sig_real * tap_real - sig_imag * tap_imag, sig_real * tap_imag + sig_imag * tap_real],
        axis=2,
    )
    long_part, waits = inverse_real(product, half, waits)
    long_part = long_part.reshape(1, count, length)
    return long_part, waits


def gather_earlier(block, shards, me):
    plane = 4 if shards % 4 == 0 else 1
    lines = shards // plane
    lane = me % plane
    level = me // plane
    stack = [block]
    for depth in range(1, lines):
        step = depth * plane
        stack.append(lax.ppermute(block, "seq", [(i, i + step) for i in range(shards - step)]))
    stack = jnp.stack(stack)
    src_level = level - jnp.arange(lines, dtype=jnp.int32)

    def origin(from_lane):
        return jnp.where(src_level >= 0, src_level * plane + from_lane, shards)

    if plane == 1:
        return stack, origin(lane)
    base = [p * plane for p in range(lines)]
    across = [(b + l, b + (l ^ 2)) for b in base for l in range(plane)]
    beside = [(b + l, b + (l ^ 1)) for b in base for l in range(plane)]
    far = lax.ppermute(stack, "seq", across)
    both = jnp.concatenate([stack, far])
    near = lax.ppermute(both, "seq", beside)
    blocks = jnp.concatenate([both, near])
    sources = jnp.concatenate(
        [origin(lane), origin(lane ^ 2), origin(lane ^ 1), origin(lane ^ 3)]
    )
    return blocks, sources

def on_device(left_stream, right_stream, gate_stream, filter_taps, w_query, w_key, w_value):
    rows, channels = left_stream.shape
    shards = lax.axis_size("seq")
    group = channels // shards
    mixed = (left_stream.astype(jnp.float32) * right_stream.astype(jnp.float32)).astype(
        jnp.bfloat16
    )
    mixed_groups = mixed.T.reshape(shards, group, rows)
    tap_groups = filter_taps.T.reshape(shards, group, rows)
    chunks = 2 if group % 16 == 0 else 1
    sub = group // chunks
    gate_groups = gate_stream.T.reshape(shards, group, rows)
    arrived = []
    for k in range(chunks):
        cut = slice(k * sub, (k + 1) * sub)
        parts = [mixed_groups[:, cut], tap_groups[:, cut]]
        if k == chunks - 1:
            parts.append(gate_groups[:, cut])
        payload = jnp.concatenate(parts, axis=1)
        arrived.append(lax.all_to_all(payload, "seq", split_axis=0, concat_axis=0, tiled=True))
    pieces = []
    previous = None
    for k in range(chunks):
        got = arrived[k]
        back = None
        if previous is not None:
            got, previous = lax.optimization_barrier((got, previous))
            back = lax.all_to_all(previous, "seq", split_axis=0, concat_axis=0, tiled=True)
        long_k, back = make_convolver(got[:, : 2 * sub], back)
        if back is not None:
            pieces.append(back)
        previous = long_k.reshape(sub, shards, rows).transpose(1, 0, 2)
    last = (got[:, 2 * sub :].astype(jnp.float32) * previous).astype(jnp.bfloat16)
    pieces.append(lax.all_to_all(last, "seq", split_axis=0, concat_axis=0, tiled=True))
    gate_parts = gate_stream.reshape(rows, shards, chunks, sub)
    outs = []
    for k, piece in enumerate(pieces):
        piece = piece.transpose(2, 0, 1)
        if k < chunks - 1:
            piece = (gate_parts[:, :, k].astype(jnp.float32) * piece).astype(jnp.bfloat16)
        outs.append(piece)
    conv_out = jnp.stack(outs, axis=2).reshape(rows, channels)
    query = jnp.dot(conv_out, w_query, preferred_element_type=jnp.float32).astype(jnp.bfloat16)
    key = jnp.dot(conv_out, w_key, preferred_element_type=jnp.float32).astype(jnp.bfloat16)
    value = jnp.dot(conv_out, w_value, preferred_element_type=jnp.float32).astype(jnp.bfloat16)
    head_size = w_query.shape[1]
    scale = 1.0 / math.sqrt(head_size)
    me = lax.axis_index("seq")
    query_pos = me * rows + jnp.arange(rows, dtype=jnp.int32)
    pairs = jnp.concatenate([key, value], axis=1)
    blocks, sources = gather_earlier(pairs, shards, me)
    keys = blocks[:, :, :head_size].reshape(-1, head_size)
    values = blocks[:, :, head_size:].reshape(-1, head_size)
    key_pos = (sources[:, None] * rows + jnp.arange(rows, dtype=jnp.int32)[None, :]).reshape(-1)
    score = jnp.einsum("qd,kd->qk", query, keys, preferred_element_type=jnp.float32) * scale
    allowed = key_pos[None, :] <= query_pos[:, None]
    masked = jnp.where(allowed, score, -1e30)
    peak = jnp.max(masked, axis=1)
    weight = jnp.where(allowed, jnp.exp(masked - peak[:, None]), 0.0)
    total = jnp.sum(weight, axis=1)
    summed = jnp.dot(weight.astype(jnp.bfloat16), values, preferred_element_type=jnp.float32)
    attended = (summed / total[:, None]).astype(jnp.bfloat16)
    return (conv_out, attended)


def solution(mesh):
    in_specs = (
        P(("groups", "seq"), None),
        P(("groups", "seq"), None),
        P(("groups", "seq"), None),
        P("seq", None),
        P(),
        P(),
        P(),
    )
    out_specs = (P(("groups", "seq"), None), P(("groups", "seq"), None))
    return jax.shard_map(
        on_device, mesh=mesh, in_specs=in_specs, out_specs=out_specs, check_vma=False
    )
```

```python
import math

import jax
import jax.numpy as jnp
from jax import lax
from jax.sharding import PartitionSpec as P

careful = lax.Precision.HIGH


def angle_table(rows, cols, period, sign):
    product = (
        lax.broadcasted_iota(jnp.int32, (rows, cols), 0)
        * lax.broadcasted_iota(jnp.int32, (rows, cols), 1)
        % period
    )
    phase = product.astype(jnp.float32) * (sign * 2.0 * math.pi / period)
    return (jnp.cos(phase), jnp.sin(phase))


def spectrum(signal):
    half, count, width = signal.shape
    outer = 2 * half
    whole = outer * width
    cos_a, sin_a = angle_table(outer, half, outer, -1.0)
    both_a = jnp.einsum(
        "kn,ncm->ckm",
        jnp.concatenate([cos_a, sin_a]),
        signal,
        precision=careful,
        preferred_element_type=jnp.float32,
    )
    real_a = both_a[:, :outer]
    imag_a = both_a[:, outer:]
    cos_t, sin_t = angle_table(outer, width, whole, -1.0)
    real_b = real_a * cos_t - imag_a * sin_t
    imag_b = real_a * sin_t + imag_a * cos_t
    cos_c, sin_c = angle_table(width, width, width, -1.0)
    rotate = jnp.concatenate(
        [
            jnp.concatenate([cos_c.T, sin_c.T], axis=1),
            jnp.concatenate([-sin_c.T, cos_c.T], axis=1),
        ]
    )
    return jnp.einsum(
        "cqn,nk->cqk", jnp.concatenate([real_b, imag_b], axis=2), rotate, precision=careful
    )


def inverse_real(product, half, waits=None):
    count, outer, double = product.shape
    width = double // 2
    whole = outer * width
    cos_c, sin_c = angle_table(width, width, width, 1.0)
    rotate = jnp.concatenate(
        [
            jnp.concatenate([cos_c.T, sin_c.T], axis=1),
            jnp.concatenate([-sin_c.T, cos_c.T], axis=1),
        ]
    )
    both_c = jnp.einsum("cqk,kn->cqn", product, rotate, precision=careful)
    if waits is not None:
        both_c, waits = lax.optimization_barrier((both_c, waits))
    real_c = both_c[:, :, :width]
    imag_c = both_c[:, :, width:]
    cos_t, sin_t = angle_table(outer, width, whole, 1.0)
    real_d = real_c * cos_t - imag_c * sin_t
    imag_d = real_c * sin_t + imag_c * cos_t
    cos_a, sin_a = angle_table(half, outer, outer, 1.0)
    result = jnp.einsum(
        "nk,ckm->cnm",
        jnp.concatenate([cos_a, -sin_a], axis=1),
        jnp.concatenate([real_d, imag_d], axis=1),
        precision=careful,
    )
    return (result / whole).reshape(count, half * width), waits


def make_convolver(both, waits=None):
    half, double, width = both.shape
    count = double // 2
    length = half * width
    spectra = spectrum(both)
    sig_real = spectra[:count, :, :width]
    sig_imag = spectra[:count, :, width:]
    tap_real = spectra[count:, :, :width]
    tap_imag = spectra[count:, :, width:]
    product = jnp.concatenate(
        [sig_real * tap_real - sig_imag * tap_imag, sig_real * tap_imag + sig_imag * tap_real],
        axis=2,
    )
    long_part, waits = inverse_real(product, half, waits)
    long_part = long_part.reshape(1, count, length)
    return long_part, waits


def gather_earlier(block, shards, me):
    plane = 4 if shards % 4 == 0 else 1
    lines = shards // plane
    lane = me % plane
    level = me // plane
    stack = [block]
    for depth in range(1, lines):
        step = depth * plane
        stack.append(lax.ppermute(block, "seq", [(i, i + step) for i in range(shards - step)]))
    stack = jnp.stack(stack)
    src_level = level - jnp.arange(lines, dtype=jnp.int32)

    def origin(from_lane):
        return jnp.where(src_level >= 0, src_level * plane + from_lane, shards)

    if plane == 1:
        return stack, origin(lane)
    base = [p * plane for p in range(lines)]
    across = [(b + l, b + (l ^ 2)) for b in base for l in range(plane)]
    beside = [(b + l, b + (l ^ 1)) for b in base for l in range(plane)]
    far = lax.ppermute(stack, "seq", across)
    both = jnp.concatenate([stack, far])
    near = lax.ppermute(both, "seq", beside)
    blocks = jnp.concatenate([both, near])
    sources = jnp.concatenate(
        [origin(lane), origin(lane ^ 2), origin(lane ^ 1), origin(lane ^ 3)]
    )
    return blocks, sources

def on_device(left_stream, right_stream, gate_stream, filter_taps, w_query, w_key, w_value):
    rows, channels = left_stream.shape
    shards = lax.axis_size("seq")
    group = channels // shards
    mixed = (left_stream.astype(jnp.float32) * right_stream.astype(jnp.float32)).astype(
        jnp.bfloat16
    )
    mixed_groups = mixed.T.reshape(shards, group, rows)
    tap_groups = filter_taps.T.reshape(shards, group, rows)
    chunks = 2 if group % 16 == 0 else 1
    sub = group // chunks
    gate_groups = gate_stream.T.reshape(shards, group, rows)
    arrived = []
    for k in range(chunks):
        cut = slice(k * sub, (k + 1) * sub)
        parts = [mixed_groups[:, cut], tap_groups[:, cut]]
        if k == 0:
            parts.append(gate_groups[:, group - sub :])
        payload = jnp.concatenate(parts, axis=1)
        arrived.append(lax.all_to_all(payload, "seq", split_axis=0, concat_axis=0, tiled=True))
    pieces = []
    previous = None
    for k in range(chunks):
        got = arrived[k]
        back = None
        if previous is not None:
            got, previous = lax.optimization_barrier((got, previous))
            back = lax.all_to_all(previous, "seq", split_axis=0, concat_axis=0, tiled=True)
        long_k, back = make_convolver(got[:, : 2 * sub], back)
        if back is not None:
            pieces.append(back)
        previous = long_k.reshape(sub, shards, rows).transpose(1, 0, 2)
    last = (arrived[0][:, 2 * sub :].astype(jnp.float32) * previous).astype(jnp.bfloat16)
    pieces.append(lax.all_to_all(last, "seq", split_axis=0, concat_axis=0, tiled=True))
    gate_parts = gate_stream.reshape(rows, shards, chunks, sub)
    outs = []
    for k, piece in enumerate(pieces):
        piece = piece.transpose(2, 0, 1)
        if k < chunks - 1:
            piece = (gate_parts[:, :, k].astype(jnp.float32) * piece).astype(jnp.bfloat16)
        outs.append(piece)
    conv_out = jnp.stack(outs, axis=2).reshape(rows, channels)
    query = jnp.dot(conv_out, w_query, preferred_element_type=jnp.float32).astype(jnp.bfloat16)
    key = jnp.dot(conv_out, w_key, preferred_element_type=jnp.float32).astype(jnp.bfloat16)
    value = jnp.dot(conv_out, w_value, preferred_element_type=jnp.float32).astype(jnp.bfloat16)
    head_size = w_query.shape[1]
    scale = 1.0 / math.sqrt(head_size)
    me = lax.axis_index("seq")
    query_pos = me * rows + jnp.arange(rows, dtype=jnp.int32)
    pairs = jnp.concatenate([key, value], axis=1)
    blocks, sources = gather_earlier(pairs, shards, me)
    keys = blocks[:, :, :head_size].reshape(-1, head_size)
    values = blocks[:, :, head_size:].reshape(-1, head_size)
    key_pos = (sources[:, None] * rows + jnp.arange(rows, dtype=jnp.int32)[None, :]).reshape(-1)
    score = jnp.einsum("qd,kd->qk", query, keys, preferred_element_type=jnp.float32) * scale
    allowed = key_pos[None, :] <= query_pos[:, None]
    masked = jnp.where(allowed, score, -1e30)
    peak = jnp.max(masked, axis=1)
    weight = jnp.where(allowed, jnp.exp(masked - peak[:, None]), 0.0)
    total = jnp.sum(weight, axis=1)
    summed = jnp.dot(weight.astype(jnp.bfloat16), values, preferred_element_type=jnp.float32)
    attended = (summed / total[:, None]).astype(jnp.bfloat16)
    return (conv_out, attended)


def solution(mesh):
    in_specs = (
        P(("groups", "seq"), None),
        P(("groups", "seq"), None),
        P(("groups", "seq"), None),
        P("seq", None),
        P(),
        P(),
        P(),
    )
    out_specs = (P(("groups", "seq"), None), P(("groups", "seq"), None))
    return jax.shard_map(
        on_device, mesh=mesh, in_specs=in_specs, out_specs=out_specs, check_vma=False
    )
```

```python
import math

import jax
import jax.numpy as jnp
from jax import lax
from jax.sharding import PartitionSpec as P

careful = lax.Precision.HIGH


def angle_table(rows, cols, period, sign):
    product = (
        lax.broadcasted_iota(jnp.int32, (rows, cols), 0)
        * lax.broadcasted_iota(jnp.int32, (rows, cols), 1)
        % period
    )
    phase = product.astype(jnp.float32) * (sign * 2.0 * math.pi / period)
    return (jnp.cos(phase), jnp.sin(phase))


def spectrum(signal):
    half, count, width = signal.shape
    outer = 2 * half
    whole = outer * width
    cos_a, sin_a = angle_table(outer, half, outer, -1.0)
    both_a = jnp.einsum(
        "kn,ncm->ckm",
        jnp.concatenate([cos_a, sin_a]),
        signal,
        precision=careful,
        preferred_element_type=jnp.float32,
    )
    real_a = both_a[:, :outer]
    imag_a = both_a[:, outer:]
    cos_t, sin_t = angle_table(outer, width, whole, -1.0)
    real_b = real_a * cos_t - imag_a * sin_t
    imag_b = real_a * sin_t + imag_a * cos_t
    cos_c, sin_c = angle_table(width, width, width, -1.0)
    rotate = jnp.concatenate(
        [
            jnp.concatenate([cos_c.T, sin_c.T], axis=1),
            jnp.concatenate([-sin_c.T, cos_c.T], axis=1),
        ]
    )
    return jnp.einsum(
        "cqn,nk->cqk", jnp.concatenate([real_b, imag_b], axis=2), rotate, precision=careful
    )


def inverse_real(product, half, waits=None):
    count, outer, double = product.shape
    width = double // 2
    whole = outer * width
    cos_c, sin_c = angle_table(width, width, width, 1.0)
    rotate = jnp.concatenate(
        [
            jnp.concatenate([cos_c.T, sin_c.T], axis=1),
            jnp.concatenate([-sin_c.T, cos_c.T], axis=1),
        ]
    )
    both_c = jnp.einsum("cqk,kn->cqn", product, rotate, precision=careful)
    if waits is not None:
        both_c, waits = lax.optimization_barrier((both_c, waits))
    real_c = both_c[:, :, :width]
    imag_c = both_c[:, :, width:]
    cos_t, sin_t = angle_table(outer, width, whole, 1.0)
    real_d = real_c * cos_t - imag_c * sin_t
    imag_d = real_c * sin_t + imag_c * cos_t
    cos_a, sin_a = angle_table(half, outer, outer, 1.0)
    result = jnp.einsum(
        "nk,ckm->cnm",
        jnp.concatenate([cos_a, -sin_a], axis=1),
        jnp.concatenate([real_d, imag_d], axis=1),
        precision=careful,
    )
    return (result / whole).reshape(count, half * width), waits


def make_convolver(both, waits=None):
    half, double, width = both.shape
    count = double // 2
    length = half * width
    spectra = spectrum(both)
    sig_real = spectra[:count, :, :width]
    sig_imag = spectra[:count, :, width:]
    tap_real = spectra[count:, :, :width]
    tap_imag = spectra[count:, :, width:]
    product = jnp.concatenate(
        [sig_real * tap_real - sig_imag * tap_imag, sig_real * tap_imag + sig_imag * tap_real],
        axis=2,
    )
    long_part, waits = inverse_real(product, half, waits)
    long_part = long_part.reshape(1, count, length)
    return long_part, waits


def gather_earlier(block, shards, me):
    plane = 4 if shards % 4 == 0 else 1
    lines = shards // plane
    lane = me % plane
    level = me // plane
    stack = [block]
    for depth in range(1, lines):
        step = depth * plane
        stack.append(lax.ppermute(block, "seq", [(i, i + step) for i in range(shards - step)]))
    stack = jnp.stack(stack)
    src_level = level - jnp.arange(lines, dtype=jnp.int32)

    def origin(from_lane):
        return jnp.where(src_level >= 0, src_level * plane + from_lane, shards)

    if plane == 1:
        return stack, origin(lane)
    base = [p * plane for p in range(lines)]
    across = [(b + l, b + (l ^ 2)) for b in base for l in range(plane)]
    beside = [(b + l, b + (l ^ 1)) for b in base for l in range(plane)]
    far = lax.ppermute(stack, "seq", across)
    both = jnp.concatenate([stack, far])
    near = lax.ppermute(both, "seq", beside)
    blocks = jnp.concatenate([both, near])
    sources = jnp.concatenate(
        [origin(lane), origin(lane ^ 2), origin(lane ^ 1), origin(lane ^ 3)]
    )
    return blocks, sources

def on_device(left_stream, right_stream, gate_stream, filter_taps, w_query, w_key, w_value):
    rows, channels = left_stream.shape
    shards = lax.axis_size("seq")
    group = channels // shards
    mixed = (left_stream.astype(jnp.float32) * right_stream.astype(jnp.float32)).astype(
        jnp.bfloat16
    )
    mixed_groups = mixed.T.reshape(shards, group, rows)
    tap_groups = filter_taps.T.reshape(shards, group, rows)
    chunks = 2 if group % 16 == 0 else 1
    sub = group // chunks
    arrived = []
    for k in range(chunks):
        cut = slice(k * sub, (k + 1) * sub)
        payload = jnp.concatenate([mixed_groups[:, cut], tap_groups[:, cut]], axis=1)
        arrived.append(lax.all_to_all(payload, "seq", split_axis=0, concat_axis=0, tiled=True))
    pieces = []
    previous = None
    for k in range(chunks):
        got = arrived[k]
        back = None
        if previous is not None:
            got, previous = lax.optimization_barrier((got, previous))
            back = lax.all_to_all(previous, "seq", split_axis=0, concat_axis=0, tiled=True)
        long_k, back = make_convolver(got, back)
        if back is not None:
            pieces.append(back)
        previous = long_k.reshape(sub, shards, rows).transpose(1, 0, 2)
    pieces.append(lax.all_to_all(previous, "seq", split_axis=0, concat_axis=0, tiled=True))
    returned = jnp.concatenate(pieces, axis=1)
    long_part = returned.reshape(channels, rows).T
    conv_out = (gate_stream.astype(jnp.float32) * long_part).astype(jnp.bfloat16)
    query = jnp.dot(conv_out, w_query, preferred_element_type=jnp.float32).astype(jnp.bfloat16)
    key = jnp.dot(conv_out, w_key, preferred_element_type=jnp.float32).astype(jnp.bfloat16)
    value = jnp.dot(conv_out, w_value, preferred_element_type=jnp.float32).astype(jnp.bfloat16)
    head_size = w_query.shape[1]
    scale = 1.0 / math.sqrt(head_size)
    me = lax.axis_index("seq")
    query_pos = me * rows + jnp.arange(rows, dtype=jnp.int32)
    pairs = jnp.concatenate([key, value], axis=1)
    blocks, sources = gather_earlier(pairs, shards, me)
    keys = blocks[:, :, :head_size]
    values = blocks[:, :, head_size:]
    key_pos = sources[:, None] * rows + jnp.arange(rows, dtype=jnp.int32)[None, :]
    score = jnp.einsum("qd,bkd->qbk", query, keys, preferred_element_type=jnp.float32) * scale
    allowed = key_pos[None, :, :] <= query_pos[:, None, None]
    masked = jnp.where(allowed, score, -1e30)
    peak = jnp.max(masked, axis=(1, 2))
    weight = jnp.where(allowed, jnp.exp(masked - peak[:, None, None]), 0.0)
    total = jnp.sum(weight, axis=(1, 2))
    summed = jnp.einsum(
        "qbk,bkd->qd", weight.astype(jnp.bfloat16), values, preferred_element_type=jnp.float32
    )
    attended = (summed / total[:, None]).astype(jnp.bfloat16)
    return (conv_out, attended)


def solution(mesh):
    in_specs = (
        P(("groups", "seq"), None),
        P(("groups", "seq"), None),
        P(("groups", "seq"), None),
        P("seq", None),
        P(),
        P(),
        P(),
    )
    out_specs = (P(("groups", "seq"), None), P(("groups", "seq"), None))
    return jax.shard_map(
        on_device, mesh=mesh, in_specs=in_specs, out_specs=out_specs, check_vma=False
    )
```

```python
import math

import jax
import jax.numpy as jnp
from jax import lax
from jax.sharding import PartitionSpec as P

careful = lax.Precision.HIGH


def angle_table(rows, cols, period, sign):
    product = (
        lax.broadcasted_iota(jnp.int32, (rows, cols), 0)
        * lax.broadcasted_iota(jnp.int32, (rows, cols), 1)
        % period
    )
    phase = product.astype(jnp.float32) * (sign * 2.0 * math.pi / period)
    return (jnp.cos(phase), jnp.sin(phase))


def spectrum(signal):
    half, count, width = signal.shape
    outer = 2 * half
    whole = outer * width
    cos_a, sin_a = angle_table(outer, half, outer, -1.0)
    both_a = jnp.einsum(
        "kn,ncm->ckm",
        jnp.concatenate([cos_a, sin_a]),
        signal,
        precision=careful,
        preferred_element_type=jnp.float32,
    )
    real_a = both_a[:, :outer]
    imag_a = both_a[:, outer:]
    cos_t, sin_t = angle_table(outer, width, whole, -1.0)
    real_b = real_a * cos_t - imag_a * sin_t
    imag_b = real_a * sin_t + imag_a * cos_t
    cos_c, sin_c = angle_table(width, width, width, -1.0)
    rotate = jnp.concatenate(
        [
            jnp.concatenate([cos_c.T, sin_c.T], axis=1),
            jnp.concatenate([-sin_c.T, cos_c.T], axis=1),
        ]
    )
    return jnp.einsum(
        "cqn,nk->cqk", jnp.concatenate([real_b, imag_b], axis=2), rotate, precision=careful
    )


def inverse_real(product, half, waits=None):
    count, outer, double = product.shape
    width = double // 2
    whole = outer * width
    cos_c, sin_c = angle_table(width, width, width, 1.0)
    rotate = jnp.concatenate(
        [
            jnp.concatenate([cos_c.T, sin_c.T], axis=1),
            jnp.concatenate([-sin_c.T, cos_c.T], axis=1),
        ]
    )
    both_c = jnp.einsum("cqk,kn->cqn", product, rotate, precision=careful)
    if waits is not None:
        both_c, waits = lax.optimization_barrier((both_c, waits))
    real_c = both_c[:, :, :width]
    imag_c = both_c[:, :, width:]
    cos_t, sin_t = angle_table(outer, width, whole, 1.0)
    real_d = real_c * cos_t - imag_c * sin_t
    imag_d = real_c * sin_t + imag_c * cos_t
    cos_a, sin_a = angle_table(half, outer, outer, 1.0)
    result = jnp.einsum(
        "nk,ckm->cnm",
        jnp.concatenate([cos_a, -sin_a], axis=1),
        jnp.concatenate([real_d, imag_d], axis=1),
        precision=careful,
    )
    return (result / whole).reshape(count, half * width), waits


def make_convolver(both, waits=None):
    half, double, width = both.shape
    count = double // 2
    length = half * width
    spectra = spectrum(both)
    sig_real = spectra[:count, :, :width]
    sig_imag = spectra[:count, :, width:]
    tap_real = spectra[count:, :, :width]
    tap_imag = spectra[count:, :, width:]
    product = jnp.concatenate(
        [sig_real * tap_real - sig_imag * tap_imag, sig_real * tap_imag + sig_imag * tap_real],
        axis=2,
    )
    long_part, waits = inverse_real(product, half, waits)
    long_part = long_part.reshape(1, count, length)
    return long_part, waits


def gather_earlier(block, shards, me):
    plane = 4 if shards % 4 == 0 else 1
    lines = shards // plane
    lane = me % plane
    level = me // plane
    stack = [block]
    for depth in range(1, lines):
        step = depth * plane
        stack.append(lax.ppermute(block, "seq", [(i, i + step) for i in range(shards - step)]))
    stack = jnp.stack(stack)
    src_level = level - jnp.arange(lines, dtype=jnp.int32)

    def origin(from_lane):
        return jnp.where(src_level >= 0, src_level * plane + from_lane, shards)

    if plane == 1:
        return stack, origin(lane)
    base = [p * plane for p in range(lines)]
    across = [(b + l, b + (l ^ 2)) for b in base for l in range(plane)]
    beside = [(b + l, b + (l ^ 1)) for b in base for l in range(plane)]
    far = lax.ppermute(stack, "seq", across)
    both = jnp.concatenate([stack, far])
    near = lax.ppermute(both, "seq", beside)
    blocks = jnp.concatenate([both, near])
    sources = jnp.concatenate(
        [origin(lane), origin(lane ^ 2), origin(lane ^ 1), origin(lane ^ 3)]
    )
    return blocks, sources

def on_device(left_stream, right_stream, gate_stream, filter_taps, w_query, w_key, w_value):
    rows, channels = left_stream.shape
    shards = lax.axis_size("seq")
    group = channels // shards
    mixed = (left_stream.astype(jnp.float32) * right_stream.astype(jnp.float32)).astype(
        jnp.bfloat16
    )
    chunks = 2 if group % 16 == 0 else 1
    sub = group // chunks
    mixed_groups = mixed.reshape(rows, shards, chunks, sub)
    tap_groups = filter_taps.reshape(rows, shards, chunks, sub)
    arrived = []
    for k in range(chunks):
        payload = jnp.concatenate(
            [mixed_groups[:, :, k].transpose(1, 2, 0), tap_groups[:, :, k].transpose(1, 2, 0)],
            axis=1,
        )
        arrived.append(lax.all_to_all(payload, "seq", split_axis=0, concat_axis=0, tiled=True))
    pieces = []
    previous = None
    for k in range(chunks):
        got = arrived[k]
        back = None
        if previous is not None:
            got, previous = lax.optimization_barrier((got, previous))
            back = lax.all_to_all(previous, "seq", split_axis=0, concat_axis=0, tiled=True)
        long_k, back = make_convolver(got, back)
        if back is not None:
            pieces.append(back)
        previous = long_k.reshape(sub, shards, rows).transpose(1, 0, 2)
    pieces.append(lax.all_to_all(previous, "seq", split_axis=0, concat_axis=0, tiled=True))
    returned = jnp.concatenate(pieces, axis=1)
    long_part = returned.reshape(channels, rows).T
    conv_out = (gate_stream.astype(jnp.float32) * long_part).astype(jnp.bfloat16)
    query = jnp.dot(conv_out, w_query, preferred_element_type=jnp.float32).astype(jnp.bfloat16)
    key = jnp.dot(conv_out, w_key, preferred_element_type=jnp.float32).astype(jnp.bfloat16)
    value = jnp.dot(conv_out, w_value, preferred_element_type=jnp.float32).astype(jnp.bfloat16)
    head_size = w_query.shape[1]
    scale = 1.0 / math.sqrt(head_size)
    me = lax.axis_index("seq")
    query_pos = me * rows + jnp.arange(rows, dtype=jnp.int32)
    pairs = jnp.concatenate([key, value], axis=1)
    blocks, sources = gather_earlier(pairs, shards, me)
    keys = blocks[:, :, :head_size]
    values = blocks[:, :, head_size:]
    key_pos = sources[:, None] * rows + jnp.arange(rows, dtype=jnp.int32)[None, :]
    score = jnp.einsum("qd,bkd->qbk", query, keys, preferred_element_type=jnp.float32) * scale
    allowed = key_pos[None, :, :] <= query_pos[:, None, None]
    masked = jnp.where(allowed, score, -1e30)
    peak = jnp.max(masked, axis=(1, 2))
    weight = jnp.where(allowed, jnp.exp(masked - peak[:, None, None]), 0.0)
    total = jnp.sum(weight, axis=(1, 2))
    summed = jnp.einsum(
        "qbk,bkd->qd", weight.astype(jnp.bfloat16), values, preferred_element_type=jnp.float32
    )
    attended = (summed / total[:, None]).astype(jnp.bfloat16)
    return (conv_out, attended)


def solution(mesh):
    in_specs = (
        P(("groups", "seq"), None),
        P(("groups", "seq"), None),
        P(("groups", "seq"), None),
        P("seq", None),
        P(),
        P(),
        P(),
    )
    out_specs = (P(("groups", "seq"), None), P(("groups", "seq"), None))
    return jax.shard_map(
        on_device, mesh=mesh, in_specs=in_specs, out_specs=out_specs, check_vma=False
    )
```

```python
import math

import jax
import jax.numpy as jnp
from jax import lax
from jax.sharding import PartitionSpec as P

careful = lax.Precision.HIGH


def angle_table(rows, cols, period, sign):
    product = (
        lax.broadcasted_iota(jnp.int32, (rows, cols), 0)
        * lax.broadcasted_iota(jnp.int32, (rows, cols), 1)
        % period
    )
    phase = product.astype(jnp.float32) * (sign * 2.0 * math.pi / period)
    return (jnp.cos(phase), jnp.sin(phase))


def spectrum(signal):
    half, count, width = signal.shape
    outer = 2 * half
    whole = outer * width
    cos_a, sin_a = angle_table(outer, half, outer, -1.0)
    both_a = jnp.einsum(
        "kn,ncm->ckm",
        jnp.concatenate([cos_a, sin_a]),
        signal,
        precision=careful,
        preferred_element_type=jnp.float32,
    )
    real_a = both_a[:, :outer]
    imag_a = both_a[:, outer:]
    cos_t, sin_t = angle_table(outer, width, whole, -1.0)
    real_b = real_a * cos_t - imag_a * sin_t
    imag_b = real_a * sin_t + imag_a * cos_t
    cos_c, sin_c = angle_table(width, width, width, -1.0)
    rotate = jnp.concatenate(
        [
            jnp.concatenate([cos_c.T, sin_c.T], axis=1),
            jnp.concatenate([-sin_c.T, cos_c.T], axis=1),
        ]
    )
    return jnp.einsum(
        "cqn,nk->cqk", jnp.concatenate([real_b, imag_b], axis=2), rotate, precision=careful
    )


def inverse_real(product, half, waits=None):
    count, outer, double = product.shape
    width = double // 2
    whole = outer * width
    cos_c, sin_c = angle_table(width, width, width, 1.0)
    rotate = jnp.concatenate(
        [
            jnp.concatenate([cos_c.T, sin_c.T], axis=1),
            jnp.concatenate([-sin_c.T, cos_c.T], axis=1),
        ]
    )
    both_c = jnp.einsum("cqk,kn->cqn", product, rotate, precision=careful)
    if waits is not None:
        both_c, waits = lax.optimization_barrier((both_c, waits))
    real_c = both_c[:, :, :width]
    imag_c = both_c[:, :, width:]
    cos_t, sin_t = angle_table(outer, width, whole, 1.0)
    real_d = real_c * cos_t - imag_c * sin_t
    imag_d = real_c * sin_t + imag_c * cos_t
    cos_a, sin_a = angle_table(half, outer, outer, 1.0)
    result = jnp.einsum(
        "nk,ckm->cnm",
        jnp.concatenate([cos_a, -sin_a], axis=1),
        jnp.concatenate([real_d, imag_d], axis=1),
        precision=careful,
    )
    return (result / whole).reshape(count, half * width), waits


def make_convolver(both, waits=None):
    half, double, width = both.shape
    count = double // 2
    length = half * width
    spectra = spectrum(both)
    sig_real = spectra[:count, :, :width]
    sig_imag = spectra[:count, :, width:]
    tap_real = spectra[count:, :, :width]
    tap_imag = spectra[count:, :, width:]
    product = jnp.concatenate(
        [sig_real * tap_real - sig_imag * tap_imag, sig_real * tap_imag + sig_imag * tap_real],
        axis=2,
    )
    long_part, waits = inverse_real(product, half, waits)
    long_part = long_part.reshape(1, count, length)
    return long_part, waits


def gather_earlier(block, shards, me):
    plane = 4 if shards % 4 == 0 else 1
    lines = shards // plane
    lane = me % plane
    level = me // plane
    stack = [block]
    for depth in range(1, lines):
        step = depth * plane
        stack.append(lax.ppermute(block, "seq", [(i, i + step) for i in range(shards - step)]))
    stack = jnp.stack(stack)
    src_level = level - jnp.arange(lines, dtype=jnp.int32)

    def origin(from_lane):
        return jnp.where(src_level >= 0, src_level * plane + from_lane, shards)

    if plane == 1:
        return stack, origin(lane)
    base = [p * plane for p in range(lines)]
    across = [(b + l, b + (l ^ 2)) for b in base for l in range(plane)]
    beside = [(b + l, b + (l ^ 1)) for b in base for l in range(plane)]
    far = lax.ppermute(stack, "seq", across)
    both = jnp.concatenate([stack, far])
    near = lax.ppermute(both, "seq", beside)
    blocks = jnp.concatenate([both, near])
    sources = jnp.concatenate(
        [origin(lane), origin(lane ^ 2), origin(lane ^ 1), origin(lane ^ 3)]
    )
    return blocks, sources

def on_device(left_stream, right_stream, gate_stream, filter_taps, w_query, w_key, w_value):
    rows, channels = left_stream.shape
    shards = lax.axis_size("seq")
    group = channels // shards
    mixed = (left_stream.astype(jnp.float32) * right_stream.astype(jnp.float32)).astype(
        jnp.bfloat16
    )
    mixed_groups = mixed.T.reshape(shards, group, rows)
    tap_groups = filter_taps.T.reshape(shards, group, rows)
    chunks = 2 if group % 16 == 0 else 1
    sub = group // chunks
    arrived = []
    for k in range(chunks):
        cut = slice(k * sub, (k + 1) * sub)
        payload = jnp.concatenate([mixed_groups[:, cut], tap_groups[:, cut]], axis=1)
        arrived.append(lax.all_to_all(payload, "seq", split_axis=0, concat_axis=0, tiled=True))
    pieces = []
    previous = None
    for k in range(chunks):
        got = arrived[k]
        back = None
        if previous is not None:
            got, previous = lax.optimization_barrier((got, previous))
            back = lax.all_to_all(previous, "seq", split_axis=0, concat_axis=0, tiled=True)
        long_k, back = make_convolver(got, back)
        if back is not None:
            pieces.append(back)
        previous = long_k.reshape(sub, shards, rows).transpose(1, 0, 2)
    pieces.append(lax.all_to_all(previous, "seq", split_axis=0, concat_axis=0, tiled=True))
    returned = jnp.concatenate(pieces, axis=1)
    long_part = returned.reshape(channels, rows).T
    conv_out = (gate_stream.astype(jnp.float32) * long_part).astype(jnp.bfloat16)
    weights = jnp.concatenate([w_query, w_key, w_value], axis=1)
    projected = jnp.dot(conv_out, weights, preferred_element_type=jnp.float32).astype(jnp.bfloat16)
    query = projected[:, : w_query.shape[1]]
    pairs = projected[:, w_query.shape[1] :]
    head_size = w_query.shape[1]
    scale = 1.0 / math.sqrt(head_size)
    me = lax.axis_index("seq")
    query_pos = me * rows + jnp.arange(rows, dtype=jnp.int32)
    blocks, sources = gather_earlier(pairs, shards, me)
    keys = blocks[:, :, :head_size]
    values = blocks[:, :, head_size:]
    key_pos = sources[:, None] * rows + jnp.arange(rows, dtype=jnp.int32)[None, :]
    score = jnp.einsum("qd,bkd->qbk", query, keys, preferred_element_type=jnp.float32) * scale
    allowed = key_pos[None, :, :] <= query_pos[:, None, None]
    masked = jnp.where(allowed, score, -1e30)
    peak = jnp.max(masked, axis=(1, 2))
    weight = jnp.where(allowed, jnp.exp(masked - peak[:, None, None]), 0.0)
    total = jnp.sum(weight, axis=(1, 2))
    summed = jnp.einsum(
        "qbk,bkd->qd", weight.astype(jnp.bfloat16), values, preferred_element_type=jnp.float32
    )
    attended = (summed / total[:, None]).astype(jnp.bfloat16)
    return (conv_out, attended)


def solution(mesh):
    in_specs = (
        P(("groups", "seq"), None),
        P(("groups", "seq"), None),
        P(("groups", "seq"), None),
        P("seq", None),
        P(),
        P(),
        P(),
    )
    out_specs = (P(("groups", "seq"), None), P(("groups", "seq"), None))
    return jax.shard_map(
        on_device, mesh=mesh, in_specs=in_specs, out_specs=out_specs, check_vma=False
    )
```

```python
import math

import jax
import jax.numpy as jnp
from jax import lax
from jax.sharding import PartitionSpec as P

careful = lax.Precision.HIGH


def angle_table(rows, cols, period, sign):
    product = (
        lax.broadcasted_iota(jnp.int32, (rows, cols), 0)
        * lax.broadcasted_iota(jnp.int32, (rows, cols), 1)
        % period
    )
    phase = product.astype(jnp.float32) * (sign * 2.0 * math.pi / period)
    return (jnp.cos(phase), jnp.sin(phase))


def spectrum(signal):
    half, count, width = signal.shape
    outer = 2 * half
    whole = outer * width
    cos_a, sin_a = angle_table(outer, half, outer, -1.0)
    both_a = jnp.einsum(
        "kn,ncm->ckm",
        jnp.concatenate([cos_a, sin_a]),
        signal,
        precision=careful,
        preferred_element_type=jnp.float32,
    )
    real_a = both_a[:, :outer]
    imag_a = both_a[:, outer:]
    cos_t, sin_t = angle_table(outer, width, whole, -1.0)
    real_b = real_a * cos_t - imag_a * sin_t
    imag_b = real_a * sin_t + imag_a * cos_t
    cos_c, sin_c = angle_table(width, width, width, -1.0)
    rotate = jnp.concatenate(
        [
            jnp.concatenate([cos_c.T, sin_c.T], axis=1),
            jnp.concatenate([-sin_c.T, cos_c.T], axis=1),
        ]
    )
    return jnp.einsum(
        "cqn,nk->cqk", jnp.concatenate([real_b, imag_b], axis=2), rotate, precision=careful
    )


def inverse_real(product, half, waits=None):
    count, outer, double = product.shape
    width = double // 2
    whole = outer * width
    cos_c, sin_c = angle_table(width, width, width, 1.0)
    rotate = jnp.concatenate(
        [
            jnp.concatenate([cos_c.T, sin_c.T], axis=1),
            jnp.concatenate([-sin_c.T, cos_c.T], axis=1),
        ]
    )
    both_c = jnp.einsum("cqk,kn->cqn", product, rotate, precision=careful)
    if waits is not None:
        both_c, waits = lax.optimization_barrier((both_c, waits))
    real_c = both_c[:, :, :width]
    imag_c = both_c[:, :, width:]
    cos_t, sin_t = angle_table(outer, width, whole, 1.0)
    real_d = real_c * cos_t - imag_c * sin_t
    imag_d = real_c * sin_t + imag_c * cos_t
    cos_a, sin_a = angle_table(half, outer, outer, 1.0)
    result = jnp.einsum(
        "nk,ckm->cnm",
        jnp.concatenate([cos_a, -sin_a], axis=1),
        jnp.concatenate([real_d, imag_d], axis=1),
        precision=careful,
    )
    return (result / whole).reshape(count, half * width), waits


def make_convolver(both, waits=None):
    half, double, width = both.shape
    count = double // 2
    length = half * width
    spectra = spectrum(both)
    sig_real = spectra[:count, :, :width]
    sig_imag = spectra[:count, :, width:]
    tap_real = spectra[count:, :, :width]
    tap_imag = spectra[count:, :, width:]
    product = jnp.concatenate(
        [sig_real * tap_real - sig_imag * tap_imag, sig_real * tap_imag + sig_imag * tap_real],
        axis=2,
    )
    long_part, waits = inverse_real(product, half, waits)
    long_part = long_part.reshape(1, count, length)
    return long_part, waits


def gather_earlier(block, shards, me):
    plane = 4 if shards % 4 == 0 else 1
    lines = shards // plane
    lane = me % plane
    level = me // plane
    stack = [block]
    for depth in range(1, lines):
        step = depth * plane
        stack.append(lax.ppermute(block, "seq", [(i, i + step) for i in range(shards - step)]))
    stack = jnp.stack(stack)
    src_level = level - jnp.arange(lines, dtype=jnp.int32)

    def origin(from_lane):
        return jnp.where(src_level >= 0, src_level * plane + from_lane, shards)

    if plane == 1:
        return stack, origin(lane)
    base = [p * plane for p in range(lines)]
    across = [(b + l, b + (l ^ 2)) for b in base for l in range(plane)]
    beside = [(b + l, b + (l ^ 1)) for b in base for l in range(plane)]
    far = lax.ppermute(stack, "seq", across)
    both = jnp.concatenate([stack, far])
    near = lax.ppermute(both, "seq", beside)
    blocks = jnp.concatenate([both, near])
    sources = jnp.concatenate(
        [origin(lane), origin(lane ^ 2), origin(lane ^ 1), origin(lane ^ 3)]
    )
    return blocks, sources

def on_device(left_stream, right_stream, gate_stream, filter_taps, w_query, w_key, w_value):
    rows, channels = left_stream.shape
    shards = lax.axis_size("seq")
    group = channels // shards
    mixed = (left_stream.astype(jnp.float32) * right_stream.astype(jnp.float32)).astype(
        jnp.bfloat16
    )
    mixed_groups = mixed.T.reshape(shards, group, rows)
    tap_groups = filter_taps.T.reshape(shards, group, rows)
    chunks = 2 if group % 16 == 0 else 1
    sub = group // chunks
    arrived = []
    for k in range(chunks):
        cut = slice(k * sub, (k + 1) * sub)
        payload = jnp.concatenate([mixed_groups[:, cut], tap_groups[:, cut]], axis=1)
        arrived.append(lax.all_to_all(payload, "seq", split_axis=0, concat_axis=0, tiled=True))
    pieces = []
    previous = None
    for k in range(chunks):
        got = arrived[k]
        back = None
        if previous is not None:
            got, previous = lax.optimization_barrier((got, previous))
            back = lax.all_to_all(previous, "seq", split_axis=0, concat_axis=0, tiled=True)
        long_k, back = make_convolver(got, back)
        if back is not None:
            pieces.append(back)
        previous = long_k.reshape(sub, shards, rows).transpose(1, 0, 2)
    pieces.append(lax.all_to_all(previous, "seq", split_axis=0, concat_axis=0, tiled=True))
    weights = jnp.concatenate([w_query, w_key, w_value], axis=1)
    gate_parts = gate_stream.reshape(rows, shards, chunks, sub)
    weight_parts = weights.reshape(shards, chunks, sub, weights.shape[1])
    outs = []
    summed_parts = None
    for k, piece in enumerate(pieces):
        long_k = piece.transpose(2, 0, 1)
        conv_k = (gate_parts[:, :, k].astype(jnp.float32) * long_k).astype(jnp.bfloat16)
        outs.append(conv_k)
        part = jnp.einsum(
            "rjc,jch->rh", conv_k, weight_parts[:, k], preferred_element_type=jnp.float32
        )
        summed_parts = part if summed_parts is None else summed_parts + part
    conv_out = jnp.stack(outs, axis=2).reshape(rows, channels)
    projected = summed_parts.astype(jnp.bfloat16)
    query = projected[:, : w_query.shape[1]]
    pairs = projected[:, w_query.shape[1] :]
    head_size = w_query.shape[1]
    scale = 1.0 / math.sqrt(head_size)
    me = lax.axis_index("seq")
    query_pos = me * rows + jnp.arange(rows, dtype=jnp.int32)
    blocks, sources = gather_earlier(pairs, shards, me)
    keys = blocks[:, :, :head_size]
    values = blocks[:, :, head_size:]
    key_pos = sources[:, None] * rows + jnp.arange(rows, dtype=jnp.int32)[None, :]
    score = jnp.einsum("qd,bkd->qbk", query, keys, preferred_element_type=jnp.float32) * scale
    allowed = key_pos[None, :, :] <= query_pos[:, None, None]
    masked = jnp.where(allowed, score, -1e30)
    peak = jnp.max(masked, axis=(1, 2))
    weight = jnp.where(allowed, jnp.exp(masked - peak[:, None, None]), 0.0)
    total = jnp.sum(weight, axis=(1, 2))
    summed = jnp.einsum(
        "qbk,bkd->qd", weight.astype(jnp.bfloat16), values, preferred_element_type=jnp.float32
    )
    attended = (summed / total[:, None]).astype(jnp.bfloat16)
    return (conv_out, attended)


def solution(mesh):
    in_specs = (
        P(("groups", "seq"), None),
        P(("groups", "seq"), None),
        P(("groups", "seq"), None),
        P("seq", None),
        P(),
        P(),
        P(),
    )
    out_specs = (P(("groups", "seq"), None), P(("groups", "seq"), None))
    return jax.shard_map(
        on_device, mesh=mesh, in_specs=in_specs, out_specs=out_specs, check_vma=False
    )
```

```python
import math

import jax
import jax.numpy as jnp
from jax import lax
from jax.sharding import PartitionSpec as P

careful = lax.Precision.HIGH


def angle_table(rows, cols, period, sign):
    product = (
        lax.broadcasted_iota(jnp.int32, (rows, cols), 0)
        * lax.broadcasted_iota(jnp.int32, (rows, cols), 1)
        % period
    )
    phase = product.astype(jnp.float32) * (sign * 2.0 * math.pi / period)
    return (jnp.cos(phase), jnp.sin(phase))


def spectrum(signal):
    half, count, width = signal.shape
    outer = 2 * half
    whole = outer * width
    cos_a, sin_a = angle_table(outer, half, outer, -1.0)
    both_a = jnp.einsum(
        "kn,ncm->ckm",
        jnp.concatenate([cos_a, sin_a]),
        signal,
        precision=careful,
        preferred_element_type=jnp.float32,
    )
    real_a = both_a[:, :outer]
    imag_a = both_a[:, outer:]
    cos_t, sin_t = angle_table(outer, width, whole, -1.0)
    real_b = real_a * cos_t - imag_a * sin_t
    imag_b = real_a * sin_t + imag_a * cos_t
    cos_c, sin_c = angle_table(width, width, width, -1.0)
    rotate = jnp.concatenate(
        [
            jnp.concatenate([cos_c.T, sin_c.T], axis=1),
            jnp.concatenate([-sin_c.T, cos_c.T], axis=1),
        ]
    )
    return jnp.einsum(
        "cqn,nk->cqk", jnp.concatenate([real_b, imag_b], axis=2), rotate, precision=careful
    )


def inverse_real(product, half, waits=None):
    count, outer, double = product.shape
    width = double // 2
    whole = outer * width
    cos_c, sin_c = angle_table(width, width, width, 1.0)
    rotate = jnp.concatenate(
        [
            jnp.concatenate([cos_c.T, sin_c.T], axis=1),
            jnp.concatenate([-sin_c.T, cos_c.T], axis=1),
        ]
    )
    both_c = jnp.einsum("cqk,kn->cqn", product, rotate, precision=careful)
    if waits is not None:
        both_c, waits = lax.optimization_barrier((both_c, waits))
    real_c = both_c[:, :, :width]
    imag_c = both_c[:, :, width:]
    cos_t, sin_t = angle_table(outer, width, whole, 1.0)
    real_d = real_c * cos_t - imag_c * sin_t
    imag_d = real_c * sin_t + imag_c * cos_t
    cos_a, sin_a = angle_table(half, outer, outer, 1.0)
    result = jnp.einsum(
        "nk,ckm->cnm",
        jnp.concatenate([cos_a, -sin_a], axis=1),
        jnp.concatenate([real_d, imag_d], axis=1),
        precision=careful,
    )
    return (result / whole).reshape(count, half * width), waits


def make_convolver(both, waits=None):
    half, double, width = both.shape
    count = double // 2
    length = half * width
    spectra = spectrum(both)
    sig_real = spectra[:count, :, :width]
    sig_imag = spectra[:count, :, width:]
    tap_real = spectra[count:, :, :width]
    tap_imag = spectra[count:, :, width:]
    product = jnp.concatenate(
        [sig_real * tap_real - sig_imag * tap_imag, sig_real * tap_imag + sig_imag * tap_real],
        axis=2,
    )
    long_part, waits = inverse_real(product, half, waits)
    long_part = long_part.reshape(1, count, length)
    return long_part, waits


def gather_earlier(block, shards, me):
    plane = 4 if shards % 4 == 0 else 1
    lines = shards // plane
    lane = me % plane
    level = me // plane
    stack = [block]
    for depth in range(1, lines):
        step = depth * plane
        stack.append(lax.ppermute(block, "seq", [(i, i + step) for i in range(shards - step)]))
    stack = jnp.stack(stack)
    src_level = level - jnp.arange(lines, dtype=jnp.int32)

    def origin(from_lane):
        return jnp.where(src_level >= 0, src_level * plane + from_lane, shards)

    if plane == 1:
        return stack, origin(lane)
    base = [p * plane for p in range(lines)]
    across = [(b + l, b + (l ^ 2)) for b in base for l in range(plane)]
    beside = [(b + l, b + (l ^ 1)) for b in base for l in range(plane)]
    far = lax.ppermute(stack, "seq", across)
    both = jnp.concatenate([stack, far])
    near = lax.ppermute(both, "seq", beside)
    blocks = jnp.concatenate([both, near])
    sources = jnp.concatenate(
        [origin(lane), origin(lane ^ 2), origin(lane ^ 1), origin(lane ^ 3)]
    )
    return blocks, sources

def on_device(left_stream, right_stream, gate_stream, filter_taps, w_query, w_key, w_value):
    rows, channels = left_stream.shape
    shards = lax.axis_size("seq")
    group = channels // shards
    mixed = (left_stream.astype(jnp.float32) * right_stream.astype(jnp.float32)).astype(
        jnp.bfloat16
    )
    mixed_groups = mixed.T.reshape(shards, group, rows)
    tap_groups = filter_taps.T.reshape(shards, group, rows)
    chunks = 2 if group % 16 == 0 else 1
    sub = group // chunks
    arrived = []
    for k in range(chunks):
        cut = slice(k * sub, (k + 1) * sub)
        payload = jnp.concatenate([mixed_groups[:, cut], tap_groups[:, cut]], axis=1)
        arrived.append(lax.all_to_all(payload, "seq", split_axis=0, concat_axis=0, tiled=True))
    pieces = []
    previous = None
    for k in range(chunks):
        got = arrived[k]
        back = None
        if previous is not None:
            got, previous = lax.optimization_barrier((got, previous))
            back = lax.all_to_all(previous, "seq", split_axis=0, concat_axis=0, tiled=True)
        long_k, back = make_convolver(got, back)
        if back is not None:
            pieces.append(back)
        previous = long_k.reshape(sub, shards, rows).transpose(1, 0, 2)
    pieces.append(lax.all_to_all(previous, "seq", split_axis=0, concat_axis=0, tiled=True))
    returned = jnp.concatenate(pieces, axis=1)
    long_part = returned.reshape(channels, rows).T
    conv_out = (gate_stream.astype(jnp.float32) * long_part).astype(jnp.bfloat16)
    weights = jnp.concatenate([w_key, w_value], axis=1)
    pairs = jnp.dot(conv_out, weights, preferred_element_type=jnp.float32).astype(jnp.bfloat16)
    query = jnp.dot(conv_out, w_query, preferred_element_type=jnp.float32).astype(jnp.bfloat16)
    head_size = w_query.shape[1]
    scale = 1.0 / math.sqrt(head_size)
    me = lax.axis_index("seq")
    query_pos = me * rows + jnp.arange(rows, dtype=jnp.int32)
    blocks, sources = gather_earlier(pairs, shards, me)
    keys = blocks[:, :, :head_size]
    values = blocks[:, :, head_size:]
    key_pos = sources[:, None] * rows + jnp.arange(rows, dtype=jnp.int32)[None, :]
    score = jnp.einsum("qd,bkd->qbk", query, keys, preferred_element_type=jnp.float32) * scale
    allowed = key_pos[None, :, :] <= query_pos[:, None, None]
    masked = jnp.where(allowed, score, -1e30)
    peak = jnp.max(masked, axis=(1, 2))
    weight = jnp.where(allowed, jnp.exp(masked - peak[:, None, None]), 0.0)
    total = jnp.sum(weight, axis=(1, 2))
    summed = jnp.einsum(
        "qbk,bkd->qd", weight.astype(jnp.bfloat16), values, preferred_element_type=jnp.float32
    )
    attended = (summed / total[:, None]).astype(jnp.bfloat16)
    return (conv_out, attended)


def solution(mesh):
    in_specs = (
        P(("groups", "seq"), None),
        P(("groups", "seq"), None),
        P(("groups", "seq"), None),
        P("seq", None),
        P(),
        P(),
        P(),
    )
    out_specs = (P(("groups", "seq"), None), P(("groups", "seq"), None))
    return jax.shard_map(
        on_device, mesh=mesh, in_specs=in_specs, out_specs=out_specs, check_vma=False
    )
```

```python
import math

import jax
import jax.numpy as jnp
from jax import lax
from jax.sharding import PartitionSpec as P

careful = lax.Precision.HIGH


def angle_table(rows, cols, period, sign):
    product = (
        lax.broadcasted_iota(jnp.int32, (rows, cols), 0)
        * lax.broadcasted_iota(jnp.int32, (rows, cols), 1)
        % period
    )
    phase = product.astype(jnp.float32) * (sign * 2.0 * math.pi / period)
    return (jnp.cos(phase), jnp.sin(phase))


def spectrum(signal):
    half, count, width = signal.shape
    outer = 2 * half
    whole = outer * width
    cos_a, sin_a = angle_table(outer, half, outer, -1.0)
    both_a = jnp.einsum(
        "kn,ncm->ckm",
        jnp.concatenate([cos_a, sin_a]),
        signal,
        precision=careful,
        preferred_element_type=jnp.float32,
    )
    real_a = both_a[:, :outer]
    imag_a = both_a[:, outer:]
    cos_t, sin_t = angle_table(outer, width, whole, -1.0)
    real_b = real_a * cos_t - imag_a * sin_t
    imag_b = real_a * sin_t + imag_a * cos_t
    cos_c, sin_c = angle_table(width, width, width, -1.0)
    rotate = jnp.concatenate(
        [
            jnp.concatenate([cos_c.T, sin_c.T], axis=1),
            jnp.concatenate([-sin_c.T, cos_c.T], axis=1),
        ]
    )
    return jnp.einsum(
        "cqn,nk->cqk", jnp.concatenate([real_b, imag_b], axis=2), rotate, precision=careful
    )


def inverse_real(product, half, waits=None):
    count, outer, double = product.shape
    width = double // 2
    whole = outer * width
    cos_c, sin_c = angle_table(width, width, width, 1.0)
    rotate = jnp.concatenate(
        [
            jnp.concatenate([cos_c.T, sin_c.T], axis=1),
            jnp.concatenate([-sin_c.T, cos_c.T], axis=1),
        ]
    )
    both_c = jnp.einsum("cqk,kn->cqn", product, rotate, precision=careful)
    if waits is not None:
        both_c, waits = lax.optimization_barrier((both_c, waits))
    real_c = both_c[:, :, :width]
    imag_c = both_c[:, :, width:]
    cos_t, sin_t = angle_table(outer, width, whole, 1.0)
    real_d = real_c * cos_t - imag_c * sin_t
    imag_d = real_c * sin_t + imag_c * cos_t
    cos_a, sin_a = angle_table(half, outer, outer, 1.0)
    result = jnp.einsum(
        "nk,ckm->cnm",
        jnp.concatenate([cos_a, -sin_a], axis=1),
        jnp.concatenate([real_d, imag_d], axis=1),
        precision=careful,
    )
    return (result / whole).reshape(count, half * width), waits


def make_convolver(both, waits=None):
    half, double, width = both.shape
    count = double // 2
    length = half * width
    spectra = spectrum(both)
    sig_real = spectra[:count, :, :width]
    sig_imag = spectra[:count, :, width:]
    tap_real = spectra[count:, :, :width]
    tap_imag = spectra[count:, :, width:]
    product = jnp.concatenate(
        [sig_real * tap_real - sig_imag * tap_imag, sig_real * tap_imag + sig_imag * tap_real],
        axis=2,
    )
    long_part, waits = inverse_real(product, half, waits)
    long_part = long_part.reshape(1, count, length)
    return long_part, waits


def gather_earlier(block, shards, me):
    plane = 4 if shards % 4 == 0 else 1
    lines = shards // plane
    lane = me % plane
    level = me // plane
    stack = [block]
    for depth in range(1, lines):
        step = depth * plane
        stack.append(lax.ppermute(block, "seq", [(i, i + step) for i in range(shards - step)]))
    stack = jnp.stack(stack)
    src_level = level - jnp.arange(lines, dtype=jnp.int32)

    def origin(from_lane):
        return jnp.where(src_level >= 0, src_level * plane + from_lane, shards)

    if plane == 1:
        return stack, origin(lane)
    base = [p * plane for p in range(lines)]
    across = [(b + l, b + (l ^ 2)) for b in base for l in range(plane)]
    beside = [(b + l, b + (l ^ 1)) for b in base for l in range(plane)]
    far = lax.ppermute(stack, "seq", across)
    both = jnp.concatenate([stack, far])
    near = lax.ppermute(both, "seq", beside)
    blocks = jnp.concatenate([both, near])
    sources = jnp.concatenate(
        [origin(lane), origin(lane ^ 2), origin(lane ^ 1), origin(lane ^ 3)]
    )
    return blocks, sources

def on_device(left_stream, right_stream, gate_stream, filter_taps, w_query, w_key, w_value):
    rows, channels = left_stream.shape
    shards = lax.axis_size("seq")
    group = channels // shards
    mixed = (left_stream.astype(jnp.float32) * right_stream.astype(jnp.float32)).astype(
        jnp.bfloat16
    )
    chunks = 2 if group % 16 == 0 else 1
    sub = group // chunks
    mixed_groups = mixed.reshape(rows, shards, chunks, sub)
    tap_groups = filter_taps.reshape(rows, shards, chunks, sub)
    arrived = []
    for k in range(chunks):
        payload = jnp.concatenate(
            [mixed_groups[:, :, k].transpose(1, 2, 0), tap_groups[:, :, k].transpose(1, 2, 0)],
            axis=1,
        )
        arrived.append(lax.all_to_all(payload, "seq", split_axis=0, concat_axis=0, tiled=True))
    pieces = []
    previous = None
    for k in range(chunks):
        got = arrived[k]
        back = None
        if previous is not None:
            got, previous = lax.optimization_barrier((got, previous))
            back = lax.all_to_all(previous, "seq", split_axis=0, concat_axis=0, tiled=True)
        long_k, back = make_convolver(got, back)
        if back is not None:
            pieces.append(back)
        previous = long_k.reshape(sub, shards, rows).transpose(1, 0, 2)
    pieces.append(lax.all_to_all(previous, "seq", split_axis=0, concat_axis=0, tiled=True))
    returned = jnp.concatenate(pieces, axis=1)
    long_part = returned.reshape(channels, rows).T
    conv_out = (gate_stream.astype(jnp.float32) * long_part).astype(jnp.bfloat16)
    weights = jnp.concatenate([w_query, w_key, w_value], axis=1)
    projected = jnp.dot(conv_out, weights, preferred_element_type=jnp.float32).astype(jnp.bfloat16)
    query = projected[:, : w_query.shape[1]]
    pairs = projected[:, w_query.shape[1] :]
    head_size = w_query.shape[1]
    scale = 1.0 / math.sqrt(head_size)
    me = lax.axis_index("seq")
    query_pos = me * rows + jnp.arange(rows, dtype=jnp.int32)
    blocks, sources = gather_earlier(pairs, shards, me)
    keys = blocks[:, :, :head_size]
    values = blocks[:, :, head_size:]
    key_pos = sources[:, None] * rows + jnp.arange(rows, dtype=jnp.int32)[None, :]
    score = jnp.einsum("qd,bkd->qbk", query, keys, preferred_element_type=jnp.float32) * scale
    allowed = key_pos[None, :, :] <= query_pos[:, None, None]
    masked = jnp.where(allowed, score, -1e30)
    peak = jnp.max(masked, axis=(1, 2))
    weight = jnp.where(allowed, jnp.exp(masked - peak[:, None, None]), 0.0)
    total = jnp.sum(weight, axis=(1, 2))
    summed = jnp.einsum(
        "qbk,bkd->qd", weight.astype(jnp.bfloat16), values, preferred_element_type=jnp.float32
    )
    attended = (summed / total[:, None]).astype(jnp.bfloat16)
    return (conv_out, attended)


def solution(mesh):
    in_specs = (
        P(("groups", "seq"), None),
        P(("groups", "seq"), None),
        P(("groups", "seq"), None),
        P("seq", None),
        P(),
        P(),
        P(),
    )
    out_specs = (P(("groups", "seq"), None), P(("groups", "seq"), None))
    return jax.shard_map(
        on_device, mesh=mesh, in_specs=in_specs, out_specs=out_specs, check_vma=False
    )
```

```python
import math

import jax
import jax.numpy as jnp
from jax import lax
from jax.sharding import PartitionSpec as P

careful = lax.Precision.HIGH


def angle_table(rows, cols, period, sign):
    product = (
        lax.broadcasted_iota(jnp.int32, (rows, cols), 0)
        * lax.broadcasted_iota(jnp.int32, (rows, cols), 1)
        % period
    )
    phase = product.astype(jnp.float32) * (sign * 2.0 * math.pi / period)
    return (jnp.cos(phase), jnp.sin(phase))


def spectrum(signal):
    half, count, width = signal.shape
    outer = 2 * half
    whole = outer * width
    cos_a, sin_a = angle_table(outer, half, outer, -1.0)
    both_a = jnp.einsum(
        "kn,ncm->ckm",
        jnp.concatenate([cos_a, sin_a]),
        signal,
        precision=careful,
        preferred_element_type=jnp.float32,
    )
    real_a = both_a[:, :outer]
    imag_a = both_a[:, outer:]
    cos_t, sin_t = angle_table(outer, width, whole, -1.0)
    real_b = real_a * cos_t - imag_a * sin_t
    imag_b = real_a * sin_t + imag_a * cos_t
    cos_c, sin_c = angle_table(width, width, width, -1.0)
    rotate = jnp.concatenate(
        [
            jnp.concatenate([cos_c.T, sin_c.T], axis=1),
            jnp.concatenate([-sin_c.T, cos_c.T], axis=1),
        ]
    )
    return jnp.einsum(
        "cqn,nk->cqk", jnp.concatenate([real_b, imag_b], axis=2), rotate, precision=careful
    )


def inverse_real(product, half, waits=None):
    count, outer, double = product.shape
    width = double // 2
    whole = outer * width
    cos_c, sin_c = angle_table(width, width, width, 1.0)
    rotate = jnp.concatenate(
        [
            jnp.concatenate([cos_c.T, sin_c.T], axis=1),
            jnp.concatenate([-sin_c.T, cos_c.T], axis=1),
        ]
    )
    both_c = jnp.einsum("cqk,kn->cqn", product, rotate, precision=careful)
    if waits is not None:
        both_c, waits = lax.optimization_barrier((both_c, waits))
    real_c = both_c[:, :, :width]
    imag_c = both_c[:, :, width:]
    cos_t, sin_t = angle_table(outer, width, whole, 1.0)
    real_d = real_c * cos_t - imag_c * sin_t
    imag_d = real_c * sin_t + imag_c * cos_t
    cos_a, sin_a = angle_table(half, outer, outer, 1.0)
    result = jnp.einsum(
        "nk,ckm->cnm",
        jnp.concatenate([cos_a, -sin_a], axis=1),
        jnp.concatenate([real_d, imag_d], axis=1),
        precision=careful,
    )
    return (result / whole).reshape(count, half * width), waits


def make_convolver(both, waits=None):
    half, double, width = both.shape
    count = double // 2
    length = half * width
    spectra = spectrum(both)
    sig_real = spectra[:count, :, :width]
    sig_imag = spectra[:count, :, width:]
    tap_real = spectra[count:, :, :width]
    tap_imag = spectra[count:, :, width:]
    product = jnp.concatenate(
        [sig_real * tap_real - sig_imag * tap_imag, sig_real * tap_imag + sig_imag * tap_real],
        axis=2,
    )
    long_part, waits = inverse_real(product, half, waits)
    long_part = long_part.reshape(1, count, length)
    return long_part, waits


def gather_earlier(block, shards, me):
    plane = 4 if shards % 4 == 0 else 1
    lines = shards // plane
    lane = me % plane
    level = me // plane
    stack = [block]
    for depth in range(1, lines):
        step = depth * plane
        stack.append(lax.ppermute(block, "seq", [(i, i + step) for i in range(shards - step)]))
    stack = jnp.stack(stack)
    src_level = level - jnp.arange(lines, dtype=jnp.int32)

    def origin(from_lane):
        return jnp.where(src_level >= 0, src_level * plane + from_lane, shards)

    if plane == 1:
        return stack, origin(lane)
    base = [p * plane for p in range(lines)]
    across = [(b + l, b + (l ^ 2)) for b in base for l in range(plane)]
    beside = [(b + l, b + (l ^ 1)) for b in base for l in range(plane)]
    far = lax.ppermute(stack, "seq", across)
    both = jnp.concatenate([stack, far])
    near = lax.ppermute(both, "seq", beside)
    blocks = jnp.concatenate([both, near])
    sources = jnp.concatenate(
        [origin(lane), origin(lane ^ 2), origin(lane ^ 1), origin(lane ^ 3)]
    )
    return blocks, sources

def on_device(left_stream, right_stream, gate_stream, filter_taps, w_query, w_key, w_value):
    rows, channels = left_stream.shape
    shards = lax.axis_size("seq")
    group = channels // shards
    mixed = (left_stream.astype(jnp.float32) * right_stream.astype(jnp.float32)).astype(
        jnp.bfloat16
    )
    mixed_groups = mixed.T.reshape(shards, group, rows)
    tap_groups = filter_taps.T.reshape(shards, group, rows)
    chunks = 2 if group % 16 == 0 else 1
    sub = group // chunks
    arrived = []
    for k in range(chunks):
        cut = slice(k * sub, (k + 1) * sub)
        payload = jnp.concatenate([mixed_groups[:, cut], tap_groups[:, cut]], axis=1)
        arrived.append(lax.all_to_all(payload, "seq", split_axis=0, concat_axis=0, tiled=True))
    pieces = []
    previous = None
    for k in range(chunks):
        got = arrived[k]
        back = None
        if previous is not None:
            got, previous = lax.optimization_barrier((got, previous))
            back = lax.all_to_all(previous, "seq", split_axis=0, concat_axis=0, tiled=True)
        long_k, back = make_convolver(got, back)
        if back is not None:
            pieces.append(back)
        previous = long_k.reshape(sub, shards, rows).transpose(1, 0, 2)
    pieces.append(lax.all_to_all(previous, "seq", split_axis=0, concat_axis=0, tiled=True))
    returned = jnp.concatenate(pieces, axis=1)
    long_part = returned.reshape(channels, rows).T
    conv_out = (gate_stream.astype(jnp.float32) * long_part).astype(jnp.bfloat16)
    weights = jnp.concatenate([w_key, w_value, w_query], axis=1)
    projected = jnp.dot(conv_out, weights, preferred_element_type=jnp.float32).astype(jnp.bfloat16)
    pairs = projected[:, : 2 * w_key.shape[1]]
    query = projected[:, 2 * w_key.shape[1] :]
    head_size = w_query.shape[1]
    scale = 1.0 / math.sqrt(head_size)
    me = lax.axis_index("seq")
    query_pos = me * rows + jnp.arange(rows, dtype=jnp.int32)
    blocks, sources = gather_earlier(pairs, shards, me)
    keys = blocks[:, :, :head_size]
    values = blocks[:, :, head_size:]
    key_pos = sources[:, None] * rows + jnp.arange(rows, dtype=jnp.int32)[None, :]
    score = jnp.einsum("qd,bkd->qbk", query, keys, preferred_element_type=jnp.float32) * scale
    allowed = key_pos[None, :, :] <= query_pos[:, None, None]
    masked = jnp.where(allowed, score, -1e30)
    peak = jnp.max(masked, axis=(1, 2))
    weight = jnp.where(allowed, jnp.exp(masked - peak[:, None, None]), 0.0)
    total = jnp.sum(weight, axis=(1, 2))
    summed = jnp.einsum(
        "qbk,bkd->qd", weight.astype(jnp.bfloat16), values, preferred_element_type=jnp.float32
    )
    attended = (summed / total[:, None]).astype(jnp.bfloat16)
    return (conv_out, attended)


def solution(mesh):
    in_specs = (
        P(("groups", "seq"), None),
        P(("groups", "seq"), None),
        P(("groups", "seq"), None),
        P("seq", None),
        P(),
        P(),
        P(),
    )
    out_specs = (P(("groups", "seq"), None), P(("groups", "seq"), None))
    return jax.shard_map(
        on_device, mesh=mesh, in_specs=in_specs, out_specs=out_specs, check_vma=False
    )
```
